128 devices in a mesh: row: 4 (over z_lo, core), col: 8 (over y, z_hi), layer: 4 (over x).
Axes of the slice: x: 4, y: 4, z: 4 (z_hi: 2, z_lo: 2; z = z_hi * 2 + z_lo), core: 2. Of those that a mesh axis runs over, the one named last changes fastest.
Arguments:
- a_tiles: bfloat16 [4, 8, 4, 32, 128, 128], P('row', 'col', 'layer'), may hold values from 0 to 1, as said below
- a_coords: int32 [4, 8, 4, 32, 2], P('row', 'col', 'layer'), may hold values from 0 to 31, as said below
- b_tiles: bfloat16 [4, 8, 4, 32, 128, 128], P('row', 'col', 'layer'), may hold values from 0 to 1, as said below
- b_coords: int32 [4, 8, 4, 32, 2], P('row', 'col', 'layer'), may hold values from 0 to 15, as said below
- out_coords: int32 [4, 8, 4, 16, 2], P('row', 'col', 'layer'), may hold values from 0 to 15, as said below
Outputs:
- flow: float32 [4, 8, 4, 16, 128, 128], P('row', 'col', 'layer')
The draws below stay inside these ranges and needn't reach their ends.
Inputs may be any that keep to these rules, and one draw needn't show every extreme that they name: `a_tiles`: every entry is positive. `b_tiles`: every entry is positive. `a_coords`: on one device, column 0 takes every value below 32 exactly once; column 1 is below 4. `b_coords`: on one device, column 1 takes every value below 16 exactly twice, with two different values of column 0; column 0 is below 8. `out_coords`: on one device, column 1 takes every value below 16 exactly once; column 0 is below 8.
All inputs are finite; a program needn't handle non-finite values.
Results may differ from the reference program's by a relative error of at most 0.0003.
Values may be sent and summed in bfloat16 or wider, within the bound.
No kernel may reach another device: no remote copies, remote signals or barrier semaphores. Data moves between devices by JAX's collectives and lax.ppermute only.
A program may use at most 192 MiB of HBM per device.

```python
import jax
import jax.numpy as jnp
from jax import lax

TILE = 128
NT = 128
RT = 32
CT = 16
KS = 32
KA = 4
KB = 8
NB = 32
KEPT = 2048
N_ROW = 4
N_COL = 8
N_LAYER = 4
DEVICES = 128


def tile_values(key, shape):
    base = jax.random.uniform(key, shape, jnp.float32, 0.2, 1.0)
    return base ** 8


def draw_a_tiles(key, part):
    values = tile_values(jax.random.fold_in(key, 5), (N_ROW, N_COL, N_LAYER, RT, TILE, TILE))
    return values.astype(jnp.bfloat16)


def draw_b_tiles(key, part):
    values = tile_values(jax.random.fold_in(key, 7), (N_ROW, N_COL, N_LAYER, NB, TILE, TILE))
    return values.astype(jnp.bfloat16)


def draw_a_coords(key, part):
    keys = jax.random.split(jax.random.fold_in(key, 11), N_ROW * N_COL * N_LAYER)

    def draw_group(group_key):
        key_rows, key_inner = jax.random.split(group_key)
        rows_drawn = jax.random.permutation(key_rows, RT).astype(jnp.int32)
        inner_drawn = jax.random.randint(key_inner, (RT,), 0, KA, dtype=jnp.int32)
        return jnp.stack([rows_drawn, inner_drawn], axis=1)
    return jax.vmap(draw_group)(keys).reshape(N_ROW, N_COL, N_LAYER, RT, 2)


def draw_b_coords(key, part):
    keys = jax.random.split(jax.random.fold_in(key, 23), N_ROW * N_COL * N_LAYER)

    def draw_group(group_key):
        key_first, key_step, key_order = jax.random.split(group_key, 3)
        first_row = jax.random.randint(key_first, (CT,), 0, KB, dtype=jnp.int32)
        step_row = jax.random.randint(key_step, (CT,), 0, KB - 1, dtype=jnp.int32)
        second_row = (first_row + 1 + step_row) % KB
        rows_all = jnp.concatenate([first_row, second_row])
        columns_all = jnp.concatenate([jnp.arange(CT, dtype=jnp.int32), jnp.arange(CT, dtype=jnp.int32)])
        order_drawn = jax.random.permutation(key_order, 2 * CT)
        return jnp.stack([rows_all[order_drawn], columns_all[order_drawn]], axis=1)
    return jax.vmap(draw_group)(keys).reshape(N_ROW, N_COL, N_LAYER, NB, 2)


def draw_out_coords(key, part):
    keys = jax.random.split(jax.random.fold_in(key, 37), N_ROW * N_COL * N_LAYER)

    def draw_group(group_key):
        key_rows, key_order = jax.random.split(group_key)
        rows_drawn = jax.random.randint(key_rows, (CT,), 0, KB, dtype=jnp.int32)
        columns_drawn = jax.random.permutation(key_order, CT).astype(jnp.int32)
        return jnp.stack([rows_drawn, columns_drawn], axis=1)
    return jax.vmap(draw_group)(keys).reshape(N_ROW, N_COL, N_LAYER, CT, 2)


def setup_inputs(seed: int = 0) -> dict:
    splits = jax.random.split(jax.random.key(seed), 6)
    a_tiles = draw_a_tiles(jax.random.fold_in(splits[5], 71), 0)
    a_coords = draw_a_coords(jax.random.fold_in(splits[5], 71), 0)
    b_tiles = draw_b_tiles(jax.random.fold_in(splits[5], 71), 0)
    b_coords = draw_b_coords(jax.random.fold_in(splits[5], 71), 0)
    out_coords = draw_out_coords(jax.random.fold_in(splits[5], 71), 0)
    return dict(a_tiles=a_tiles, a_coords=a_coords, b_tiles=b_tiles, b_coords=b_coords, out_coords=out_coords)


def reference(a_tiles, a_coords, b_tiles, b_coords, out_coords):
    tile_size = a_tiles.shape[-1]
    row_index = jnp.arange(N_ROW, dtype=jnp.int32)[:, None, None, None]
    col_index = jnp.arange(N_COL, dtype=jnp.int32)[None, :, None, None]
    layer_index = jnp.arange(N_LAYER, dtype=jnp.int32)[None, None, :, None]
    a_row = (row_index * RT + a_coords[..., 0]).reshape(-1)
    a_inner = (layer_index * KS + col_index * KA + a_coords[..., 1]).reshape(-1)
    a_group = jnp.broadcast_to(col_index * N_LAYER + layer_index, a_coords.shape[:4]).reshape(-1)
    a_count = a_row.shape[0]
    a_slots = jnp.arange(a_count, dtype=jnp.int32)
    a_table = jnp.zeros((NT, N_COL * N_LAYER), jnp.int32).at[a_row, a_group].set(a_slots)
    k_table = jnp.zeros((NT, N_COL * N_LAYER), jnp.int32).at[a_row, a_group].set(a_inner)
    a_flat = a_tiles.reshape(-1, tile_size, tile_size)
    b_inner = (layer_index * KS + row_index * KB + b_coords[..., 0]).reshape(-1)
    b_column = (col_index * CT + b_coords[..., 1]).reshape(-1)
    b_count = b_inner.shape[0]
    b_table = jnp.full((NT, NT), b_count, jnp.int32).at[b_inner, b_column].set(jnp.arange(b_count, dtype=jnp.int32))
    b_flat = jnp.concatenate([b_tiles.reshape(-1, tile_size, tile_size), jnp.zeros((1, tile_size, tile_size), jnp.bfloat16)], axis=0)
    out_row = (row_index * RT + layer_index * KB + out_coords[..., 0]).reshape(DEVICES, CT)
    out_column = (col_index * CT + out_coords[..., 1]).reshape(DEVICES, CT)

    def group_tiles(pair):
        rows_here, cols_here = pair
        a_ids = a_table[rows_here]
        k_ids = k_table[rows_here]
        b_ids = b_table[k_ids, cols_here[:, None]]
        left = a_flat[a_ids].astype(jnp.float32)
        right = b_flat[b_ids].astype(jnp.float32)
        product = jnp.einsum("nmxy,nmyz->nxz", left, right)
        return product * product

    squared = lax.map(group_tiles, (out_row, out_column)).reshape(-1, tile_size, tile_size)
    columns_flat = out_column.reshape(-1)
    column_part = jnp.sum(squared, axis=1)
    column_total = jax.ops.segment_sum(column_part, columns_flat, num_segments=NT)
    factor = jnp.float32(KEPT) / column_total
    flow = squared * factor[columns_flat][:, None, :]
    return flow.reshape(N_ROW, N_COL, N_LAYER, CT, tile_size, tile_size)
```

```python
import functools

import jax
import jax.numpy as jnp
from jax import lax
from jax.experimental import pallas as pl
from jax.experimental.pallas import tpu as pltpu
from jax.sharding import PartitionSpec as P

KA = 4


def kept_partial_kernel(midx_ref, gidx_ref, flow_ref, graph_ref, out_ref, *, n_out, n_grp):
    tile = out_ref.shape[-1]

    def body(t, carry):
        out_ref[t] = jnp.zeros((tile, tile), jnp.float32)
        for c in range(n_grp):
            g = gidx_ref[t * n_grp + c]

            @pl.when(g >= 0)
            def _():
                left = flow_ref[midx_ref[t * n_grp + c]]
                right = graph_ref[g]
                out_ref[t] += jnp.dot(left, right, preferred_element_type=jnp.float32)

        return carry

    lax.fori_loop(0, n_out, body, 0)


def kept_partials(midx, gidx, flow_flat, graph_flat, n_out, n_grp):
    tile = flow_flat.shape[-1]
    kernel = functools.partial(kept_partial_kernel, n_out=n_out, n_grp=n_grp)
    return pl.pallas_call(
        kernel,
        out_shape=jax.ShapeDtypeStruct((n_out, tile, tile), jnp.float32),
        in_specs=[
            pl.BlockSpec(memory_space=pltpu.SMEM),
            pl.BlockSpec(memory_space=pltpu.SMEM),
            pl.BlockSpec(memory_space=pltpu.VMEM),
            pl.BlockSpec(memory_space=pltpu.VMEM),
        ],
        out_specs=pl.BlockSpec(memory_space=pltpu.VMEM),
    )(midx, gidx, flow_flat, graph_flat)


def local(a_tiles, a_coords, b_tiles, b_coords, out_coords):
    tile_size = a_tiles.shape[-1]
    rows_panel = a_tiles.shape[3]
    col_count = lax.axis_size("col")
    row_count = lax.axis_size("row")
    layer_count = lax.axis_size("layer")
    a_span = KA
    b_span = KA * col_count // row_count
    quarter = rows_panel // layer_count
    col_tiles = out_coords.shape[3]
    n_b = b_tiles.shape[3]

    graph_tiles = lax.all_gather(b_tiles[0, 0, 0], "row", axis=0, tiled=True)
    graph_coords = lax.all_gather(b_coords[0, 0, 0][None], "row", axis=0, tiled=True)
    flow_tiles = lax.all_gather(a_tiles[0, 0, 0], "col", axis=0, tiled=True)
    flow_coords = lax.all_gather(a_coords[0, 0, 0][None], "col", axis=0, tiled=True)
    kept_all = lax.all_gather(out_coords[0, 0, 0][None], "layer", axis=0, tiled=True)

    n_out = layer_count * col_tiles
    kept_row = (jnp.arange(layer_count, dtype=jnp.int32)[:, None] * quarter + kept_all[:, :, 0]).reshape(n_out)
    kept_col = kept_all[:, :, 1].reshape(n_out)

    a_rows = flow_coords[:, :, 0]
    a_inner = flow_coords[:, :, 1]
    match_a = a_rows[None, :, :] == kept_row[:, None, None]
    slot_a = jnp.argmax(match_a, axis=2).astype(jnp.int32)
    grp = jnp.arange(col_count, dtype=jnp.int32)
    midx = grp[None, :] * rows_panel + slot_a
    inner = jnp.take_along_axis(a_inner[None, :, :], slot_a[:, :, None], axis=2)[:, :, 0]
    k_layer = grp[None, :] * a_span + inner
    b_owner = k_layer // b_span
    b_row = k_layer % b_span
    owner_coords = graph_coords[b_owner]
    match_b = (owner_coords[..., 0] == b_row[..., None]) & (owner_coords[..., 1] == kept_col[:, None, None])
    slot_b = jnp.argmax(match_b, axis=2).astype(jnp.int32)
    gidx = jnp.where(jnp.any(match_b, axis=2), b_owner * n_b + slot_b, -1)

    flow_flat = flow_tiles.reshape(-1, tile_size, tile_size)
    graph_flat = graph_tiles.reshape(-1, tile_size, tile_size)
    partial_sum = kept_partials(
        midx.reshape(-1), gidx.reshape(-1).astype(jnp.int32), flow_flat, graph_flat, n_out, col_count
    )
    kept_tiles = lax.psum_scatter(partial_sum, "layer", scatter_dimension=0, tiled=True)

    kept_cols = out_coords[0, 0, 0, :, 1]
    squared = kept_tiles * kept_tiles
    column_part = jnp.sum(squared, axis=1)
    local_mass = jnp.zeros_like(column_part).at[kept_cols].set(column_part)
    column_total = lax.psum(local_mass, ("row", "layer"))
    factor = jnp.float32(row_count * layer_count * tile_size) / column_total
    flow = squared * factor[kept_cols][:, None, :]
    return flow.reshape(1, 1, 1, col_tiles, tile_size, tile_size)


def solution(mesh):
    in_specs = (
        P("row", "col", "layer", None, None, None),
        P("row", "col", "layer", None, None),
        P("row", "col", "layer", None, None, None),
        P("row", "col", "layer", None, None),
        P("row", "col", "layer", None, None),
    )
    out_specs = P("row", "col", "layer", None, None, None)
    return jax.shard_map(local, mesh=mesh, in_specs=in_specs, out_specs=out_specs, check_vma=False)
```

```python
import functools

import jax
import jax.numpy as jnp
from jax import lax
from jax.experimental import pallas as pl
from jax.experimental.pallas import tpu as pltpu
from jax.sharding import PartitionSpec as P

KA = 4


def kept_partial_kernel(midx_ref, gidx_ref, flow_ref, graph_ref, out_ref, *, n_out, n_grp):
    tile = out_ref.shape[-1]

    def body(t, carry):
        out_ref[t] = jnp.zeros((tile, tile), jnp.float32)
        for c in range(n_grp):
            g = gidx_ref[t * n_grp + c]

            @pl.when(g >= 0)
            def _():
                left = flow_ref[midx_ref[t * n_grp + c]]
                right = graph_ref[g]
                out_ref[t] += jnp.dot(left, right, preferred_element_type=jnp.float32)

        return carry

    lax.fori_loop(0, n_out, body, 0)


def kept_partials(midx, gidx, flow_flat, graph_flat, n_out, n_grp):
    tile = flow_flat.shape[-1]
    kernel = functools.partial(kept_partial_kernel, n_out=n_out, n_grp=n_grp)
    return pl.pallas_call(
        kernel,
        out_shape=jax.ShapeDtypeStruct((n_out, tile, tile), jnp.float32),
        in_specs=[
            pl.BlockSpec(memory_space=pltpu.SMEM),
            pl.BlockSpec(memory_space=pltpu.SMEM),
            pl.BlockSpec(memory_space=pltpu.VMEM),
            pl.BlockSpec(memory_space=pltpu.VMEM),
        ],
        out_specs=pl.BlockSpec(memory_space=pltpu.VMEM),
    )(midx, gidx, flow_flat, graph_flat)


def butterfly_sum(x, axis, n):
    d = 1
    while d < n:
        x = x + lax.ppermute(x, axis, [(i, i ^ d) for i in range(n)])
        d *= 2
    return x


def local(a_tiles, a_coords, b_tiles, b_coords, out_coords):
    tile_size = a_tiles.shape[-1]
    rows_panel = a_tiles.shape[3]
    col_count = lax.axis_size("col")
    row_count = lax.axis_size("row")
    layer_count = lax.axis_size("layer")
    a_span = KA
    b_span = KA * col_count // row_count
    quarter = rows_panel // layer_count
    col_tiles = out_coords.shape[3]
    n_b = b_tiles.shape[3]

    my_row = lax.axis_index("row")
    graph_parts = [b_tiles[0, 0, 0]] + [
        lax.ppermute(b_tiles[0, 0, 0], "row", [(i, (i + s) % row_count) for i in range(row_count)])
        for s in range(1, row_count)
    ]
    graph_tiles = jnp.concatenate(graph_parts, axis=0)
    graph_coords = lax.all_gather(b_coords[0, 0, 0][None], "row", axis=0, tiled=True)
    flow_tiles = lax.all_gather(a_tiles[0, 0, 0], "col", axis=0, tiled=True)
    flow_coords = lax.all_gather(a_coords[0, 0, 0][None], "col", axis=0, tiled=True)
    kept_all = lax.all_gather(out_coords[0, 0, 0][None], "layer", axis=0, tiled=True)

    n_out = layer_count * col_tiles
    kept_row = (jnp.arange(layer_count, dtype=jnp.int32)[:, None] * quarter + kept_all[:, :, 0]).reshape(n_out)
    kept_col = kept_all[:, :, 1].reshape(n_out)

    a_rows = flow_coords[:, :, 0]
    a_inner = flow_coords[:, :, 1]
    match_a = a_rows[None, :, :] == kept_row[:, None, None]
    slot_a = jnp.argmax(match_a, axis=2).astype(jnp.int32)
    grp = jnp.arange(col_count, dtype=jnp.int32)
    midx = grp[None, :] * rows_panel + slot_a
    inner = jnp.take_along_axis(a_inner[None, :, :], slot_a[:, :, None], axis=2)[:, :, 0]
    k_layer = grp[None, :] * a_span + inner
    b_owner = k_layer // b_span
    b_row = k_layer % b_span
    owner_coords = graph_coords[b_owner]
    match_b = (owner_coords[..., 0] == b_row[..., None]) & (owner_coords[..., 1] == kept_col[:, None, None])
    slot_b = jnp.argmax(match_b, axis=2).astype(jnp.int32)
    b_part = (my_row - b_owner) % row_count
    gidx = jnp.where(jnp.any(match_b, axis=2), b_part * n_b + slot_b, -1)

    flow_flat = flow_tiles.reshape(-1, tile_size, tile_size)
    graph_flat = graph_tiles.reshape(-1, tile_size, tile_size)
    partial_sum = kept_partials(
        midx.reshape(-1), gidx.reshape(-1).astype(jnp.int32), flow_flat, graph_flat, n_out, col_count
    )
    kept_tiles = lax.psum_scatter(partial_sum, "layer", scatter_dimension=0, tiled=True)

    kept_cols = out_coords[0, 0, 0, :, 1]
    squared = kept_tiles * kept_tiles
    column_part = jnp.sum(squared, axis=1)
    local_mass = jnp.zeros_like(column_part).at[kept_cols].set(column_part)
    column_total = butterfly_sum(butterfly_sum(local_mass, "row", row_count), "layer", layer_count)
    factor = jnp.float32(row_count * layer_count * tile_size) / column_total
    flow = squared * factor[kept_cols][:, None, :]
    return flow.reshape(1, 1, 1, col_tiles, tile_size, tile_size)


def solution(mesh):
    in_specs = (
        P("row", "col", "layer", None, None, None),
        P("row", "col", "layer", None, None),
        P("row", "col", "layer", None, None, None),
        P("row", "col", "layer", None, None),
        P("row", "col", "layer", None, None),
    )
    out_specs = P("row", "col", "layer", None, None, None)
    return jax.shard_map(local, mesh=mesh, in_specs=in_specs, out_specs=out_specs, check_vma=False)
```

```python
import functools

import jax
import jax.numpy as jnp
from jax import lax
from jax.experimental import pallas as pl
from jax.experimental.pallas import tpu as pltpu
from jax.sharding import PartitionSpec as P

KA = 4
PAD = 16


def kept_partial_kernel(mrow_ref, grow_ref, flow_ref, graph_ref, out_ref, *, n_out, n_grp, m_stride):
    tile = out_ref.shape[-1]

    def body(t, carry):
        out_ref[t] = jnp.zeros((tile, tile), jnp.float32)
        m_off = mrow_ref[t]
        for c in range(n_grp):
            g_off = grow_ref[t * n_grp + c]

            @pl.when(g_off >= 0)
            def _():
                left = flow_ref[pl.ds(pl.multiple_of(c * m_stride + m_off, PAD), tile), :]
                right = graph_ref[pl.ds(pl.multiple_of(g_off, PAD), tile), :]
                out_ref[t] += jnp.dot(left, right, preferred_element_type=jnp.float32)

        return carry

    lax.fori_loop(0, n_out, body, 0)


def kept_partials(mrow, grow, flow_flat, graph_flat, n_out, n_grp, m_stride):
    tile = flow_flat.shape[-1]
    kernel = functools.partial(kept_partial_kernel, n_out=n_out, n_grp=n_grp, m_stride=m_stride)
    return pl.pallas_call(
        kernel,
        out_shape=jax.ShapeDtypeStruct((n_out, tile, tile), jnp.float32),
        in_specs=[
            pl.BlockSpec(memory_space=pltpu.SMEM),
            pl.BlockSpec(memory_space=pltpu.SMEM),
            pl.BlockSpec(memory_space=pltpu.VMEM),
            pl.BlockSpec(memory_space=pltpu.VMEM),
        ],
        out_specs=pl.BlockSpec(memory_space=pltpu.VMEM),
        cost_estimate=pl.CostEstimate(
            flops=2 * n_out * n_grp * tile**3,
            transcendentals=0,
            bytes_accessed=2 * (flow_flat.size + graph_flat.size) + 4 * n_out * tile * tile,
        ),
    )(mrow, grow, flow_flat, graph_flat)


def butterfly_sum(x, axis, n):
    d = 1
    while d < n:
        x = x + lax.ppermute(x, axis, [(i, i ^ d) for i in range(n)])
        d *= 2
    return x


def shifted(x, axis, n):
    return [x] + [lax.ppermute(x, axis, [(i, (i + s) % n) for i in range(n)]) for s in range(1, n)]


def pack_rows(tiles, rows):
    tile = tiles.shape[-1]
    extra = jnp.zeros((PAD, tile), jnp.bfloat16)
    extra = extra.at[: rows.shape[0], : rows.shape[1]].set(rows.astype(jnp.bfloat16))
    return jnp.concatenate([tiles.reshape(-1, tile), extra], axis=0)


def local(a_tiles, a_coords, b_tiles, b_coords, out_coords):
    tile = a_tiles.shape[-1]
    rows_panel = a_tiles.shape[3]
    col_count = lax.axis_size("col")
    row_count = lax.axis_size("row")
    layer_count = lax.axis_size("layer")
    b_span = KA * col_count // row_count
    quarter = rows_panel // layer_count
    col_tiles = out_coords.shape[3]
    n_b = b_tiles.shape[3]
    my_row = lax.axis_index("row")
    my_layer = lax.axis_index("layer")

    graph_parts = shifted(pack_rows(b_tiles[0, 0, 0], b_coords[0, 0, 0].T), "row", row_count)
    g_stride = n_b * tile + PAD
    graph_flat = jnp.concatenate(graph_parts, axis=0)
    graph_coords = jnp.stack([p[n_b * tile : n_b * tile + 2, :n_b] for p in graph_parts]).astype(jnp.int32)
    kept_parts = jnp.stack(shifted(out_coords[0, 0, 0], "layer", layer_count))

    a_rows = a_coords[0, 0, 0, :, 0]
    a_inner = a_coords[0, 0, 0, :, 1]
    row_ids = jnp.arange(rows_panel, dtype=jnp.int32)
    slot_of_row = jnp.argmax(a_rows[None, :] == row_ids[:, None], axis=1).astype(jnp.int32)
    grp = jnp.arange(col_count, dtype=jnp.int32)
    m_stride = quarter * tile + PAD

    total = None
    for s in range(1, layer_count + 1):
        q = (my_layer + s) % layer_count
        slots = lax.dynamic_slice_in_dim(slot_of_row, q * quarter, quarter)
        packed = pack_rows(a_tiles[0, 0, 0][slots], a_inner[slots][None, :])
        flow_all = lax.all_gather(packed, "col", axis=0, tiled=False)
        inner_all = flow_all[:, quarter * tile, :quarter].astype(jnp.int32)
        kept_q = kept_parts[(my_layer - q) % layer_count]
        kept_r = kept_q[:, 0]
        kept_c = kept_q[:, 1]
        inner = inner_all[:, kept_r].T
        k_layer = grp[None, :] * KA + inner
        b_owner = k_layer // b_span
        b_row = k_layer % b_span
        b_part = (my_row - b_owner) % row_count
        owner_coords = graph_coords[b_part]
        match_b = (owner_coords[:, :, 0, :] == b_row[..., None]) & (owner_coords[:, :, 1, :] == kept_c[:, None, None])
        slot_b = jnp.argmax(match_b, axis=2).astype(jnp.int32)
        grow = jnp.where(jnp.any(match_b, axis=2), b_part * g_stride + slot_b * tile, -1)
        partial = kept_partials(
            (kept_r * tile).astype(jnp.int32),
            grow.reshape(-1).astype(jnp.int32),
            flow_all.reshape(-1, tile),
            graph_flat,
            col_tiles,
            col_count,
            m_stride,
        )
        if s < layer_count:
            partial = lax.ppermute(partial, "layer", [(i, (i + s) % layer_count) for i in range(layer_count)])
        total = partial if total is None else total + partial

    kept_cols = out_coords[0, 0, 0, :, 1]
    squared = total * total
    column_part = jnp.sum(squared, axis=1)
    local_mass = jnp.zeros_like(column_part).at[kept_cols].set(column_part)
    column_total = butterfly_sum(butterfly_sum(local_mass, "row", row_count), "layer", layer_count)
    factor = jnp.float32(row_count * layer_count * tile) / column_total
    flow = squared * factor[kept_cols][:, None, :]
    return flow.reshape(1, 1, 1, col_tiles, tile, tile)


def solution(mesh):
    in_specs = (
        P("row", "col", "layer", None, None, None),
        P("row", "col", "layer", None, None),
        P("row", "col", "layer", None, None, None),
        P("row", "col", "layer", None, None),
        P("row", "col", "layer", None, None),
    )
    out_specs = P("row", "col", "layer", None, None, None)
    return jax.shard_map(local, mesh=mesh, in_specs=in_specs, out_specs=out_specs, check_vma=False)
```

```python
import functools

import jax
import jax.numpy as jnp
from jax import lax
from jax.experimental import pallas as pl
from jax.experimental.pallas import tpu as pltpu
from jax.sharding import PartitionSpec as P

KA = 4


def column_kernel(goff_ref, moff_ref, oidx_ref, flow_ref, graph_ref, out_ref, lhs_ref, rhs_ref, *, n_q, n_g):
    tile = out_ref.shape[-1]
    n_col = out_ref.shape[0] // n_q

    def body(j, carry):
        for g in range(n_g):
            g_off = pl.multiple_of(goff_ref[j * n_g + g], tile)
            rhs_ref[pl.ds(g * tile, tile), :] = graph_ref[pl.ds(g_off, tile), :]
        for q in range(n_q):
            for g in range(n_g):
                m_off = moff_ref[(j * n_q + q) * n_g + g]
                left = flow_ref[pl.ds(pl.multiple_of(jnp.maximum(m_off, 0), tile), tile), :]
                left = jnp.where(m_off >= 0, left, jnp.zeros_like(left))
                lhs_ref[pl.ds(q * tile, tile), pl.ds(g * tile, tile)] = left
        res = jnp.dot(lhs_ref[...], rhs_ref[...], preferred_element_type=jnp.float32)
        for q in range(n_q):
            out_ref[oidx_ref[j * n_q + q]] = res[q * tile : (q + 1) * tile]
        return carry

    lax.fori_loop(0, n_col, body, 0)


def kept_partials(goff, moff, oidx, flow_flat, graph_flat, n_out, n_q, n_g):
    tile = flow_flat.shape[-1]
    kernel = functools.partial(column_kernel, n_q=n_q, n_g=n_g)
    return pl.pallas_call(
        kernel,
        out_shape=jax.ShapeDtypeStruct((n_out, tile, tile), jnp.float32),
        in_specs=[
            pl.BlockSpec(memory_space=pltpu.SMEM),
            pl.BlockSpec(memory_space=pltpu.SMEM),
            pl.BlockSpec(memory_space=pltpu.SMEM),
            pl.BlockSpec(memory_space=pltpu.VMEM),
            pl.BlockSpec(memory_space=pltpu.VMEM),
        ],
        out_specs=pl.BlockSpec(memory_space=pltpu.VMEM),
        scratch_shapes=[
            pltpu.VMEM((n_q * tile, n_g * tile), jnp.bfloat16),
            pltpu.VMEM((n_g * tile, tile), jnp.bfloat16),
        ],
        compiler_params=pltpu.CompilerParams(vmem_limit_bytes=48 * 1024 * 1024),
        cost_estimate=pl.CostEstimate(
            flops=2 * n_out * n_g * tile**3,
            transcendentals=0,
            bytes_accessed=2 * (flow_flat.size + graph_flat.size) + 4 * n_out * tile * tile,
        ),
    )(goff, moff, oidx, flow_flat, graph_flat)


def butterfly_sum(x, axis, n):
    d = 1
    while d < n:
        x = x + lax.ppermute(x, axis, [(i, i ^ d) for i in range(n)])
        d *= 2
    return x


def first_two(mask):
    n = mask.shape[-1]
    lo = jnp.argmax(mask, axis=-1).astype(jnp.int32)
    hi = (n - 1 - jnp.argmax(mask[..., ::-1], axis=-1)).astype(jnp.int32)
    return lo, hi


def local(a_tiles, a_coords, b_tiles, b_coords, out_coords):
    tile = a_tiles.shape[-1]
    rows_panel = a_tiles.shape[3]
    col_count = lax.axis_size("col")
    row_count = lax.axis_size("row")
    layer_count = lax.axis_size("layer")
    b_span = KA * col_count // row_count
    quarter = rows_panel // layer_count
    col_tiles = out_coords.shape[3]
    n_b = b_tiles.shape[3]
    my_row = lax.axis_index("row")

    graph_parts = [b_tiles[0, 0, 0]] + [
        lax.ppermute(b_tiles[0, 0, 0], "row", [(i, (i + s) % row_count) for i in range(row_count)])
        for s in range(1, row_count)
    ]
    graph_tiles = jnp.concatenate(graph_parts, axis=0)
    graph_coords = lax.all_gather(b_coords[0, 0, 0][None], "row", axis=0, tiled=True)
    flow_tiles = lax.all_gather(a_tiles[0, 0, 0], "col", axis=0, tiled=True)
    flow_coords = lax.all_gather(a_coords[0, 0, 0][None], "col", axis=0, tiled=True)
    kept_all = lax.all_gather(out_coords[0, 0, 0][None], "layer", axis=0, tiled=True)

    n_out = layer_count * col_tiles
    col_ids = jnp.arange(col_tiles, dtype=jnp.int32)
    part_ids = jnp.arange(row_count, dtype=jnp.int32)
    owner_of_part = (my_row - part_ids) % row_count
    coords_by_part = graph_coords[owner_of_part]
    in_col = coords_by_part[:, None, :, 1] == col_ids[None, :, None]
    lo, hi = first_two(in_col)
    g_slot = jnp.stack([lo, hi], axis=2)
    g_b0 = jnp.take_along_axis(
        jnp.broadcast_to(coords_by_part[:, None, :, 0], in_col.shape), g_slot, axis=2
    )
    g_inner = owner_of_part[:, None, None] * b_span + g_b0
    goff = ((part_ids[:, None, None] * n_b + g_slot) * tile).transpose(1, 0, 2).reshape(col_tiles, -1)
    g_inner = g_inner.transpose(1, 0, 2).reshape(col_tiles, -1)
    n_g = goff.shape[1]

    kept_here = kept_all[:, None, :, 1] == col_ids[None, :, None]
    kept_pos = jnp.argmax(kept_here, axis=2).astype(jnp.int32)
    kept_row0 = jnp.take_along_axis(kept_all[:, :, 0], kept_pos, axis=1)
    q_ids = jnp.arange(layer_count, dtype=jnp.int32)
    kept_row = q_ids[:, None] * quarter + kept_row0
    oidx = (q_ids[:, None] * col_tiles + kept_pos).T

    a_rows = flow_coords[:, :, 0]
    a_inner = flow_coords[:, :, 1]
    grp = g_inner // KA
    want = g_inner % KA
    rows_q = kept_row.T
    slot_a = jnp.argmax(
        a_rows[grp[:, None, :], :] == rows_q[:, :, None, None], axis=3
    ).astype(jnp.int32)
    have = a_inner[grp[:, None, :], slot_a] == want[:, None, :]
    moff = jnp.where(have, (grp[:, None, :] * rows_panel + slot_a) * tile, -1)

    flow_flat = flow_tiles.reshape(-1, tile)
    graph_flat = graph_tiles.reshape(-1, tile)
    partial_sum = kept_partials(
        goff.reshape(-1).astype(jnp.int32),
        moff.reshape(-1).astype(jnp.int32),
        oidx.reshape(-1).astype(jnp.int32),
        flow_flat,
        graph_flat,
        n_out,
        layer_count,
        n_g,
    )
    kept_tiles = lax.psum_scatter(partial_sum, "layer", scatter_dimension=0, tiled=True)

    kept_cols = out_coords[0, 0, 0, :, 1]
    squared = kept_tiles * kept_tiles
    column_part = jnp.sum(squared, axis=1)
    local_mass = jnp.zeros_like(column_part).at[kept_cols].set(column_part)
    column_total = butterfly_sum(butterfly_sum(local_mass, "row", row_count), "layer", layer_count)
    factor = jnp.float32(row_count * layer_count * tile) / column_total
    flow = squared * factor[kept_cols][:, None, :]
    return flow.reshape(1, 1, 1, col_tiles, tile, tile)


def solution(mesh):
    in_specs = (
        P("row", "col", "layer", None, None, None),
        P("row", "col", "layer", None, None),
        P("row", "col", "layer", None, None, None),
        P("row", "col", "layer", None, None),
        P("row", "col", "layer", None, None),
    )
    out_specs = P("row", "col", "layer", None, None, None)
    return jax.shard_map(local, mesh=mesh, in_specs=in_specs, out_specs=out_specs, check_vma=False)
```

```python
import functools

import jax
import jax.numpy as jnp
from jax import lax
from jax.experimental import pallas as pl
from jax.experimental.pallas import tpu as pltpu
from jax.sharding import PartitionSpec as P

KA = 4


def column_kernel(goff_ref, moff_ref, oidx_ref, flow_ref, graph_ref, out_ref, lhs_ref, rhs_ref, *, n_q, n_g):
    tile = out_ref.shape[-1]
    n_col = out_ref.shape[0] // n_q

    def body(j, carry):
        for g in range(n_g):
            g_off = pl.multiple_of(goff_ref[j * n_g + g], tile)
            rhs_ref[pl.ds(g * tile, tile), :] = graph_ref[pl.ds(g_off, tile), :]
        for q in range(n_q):
            for g in range(n_g):
                m_off = moff_ref[(j * n_q + q) * n_g + g]
                left = flow_ref[pl.ds(pl.multiple_of(jnp.maximum(m_off, 0), tile), tile), :]
                left = jnp.where(m_off >= 0, left, jnp.zeros_like(left))
                lhs_ref[pl.ds(q * tile, tile), pl.ds(g * tile, tile)] = left
        res = jnp.dot(lhs_ref[...], rhs_ref[...], preferred_element_type=jnp.float32)
        for q in range(n_q):
            out_ref[oidx_ref[j * n_q + q]] = res[q * tile : (q + 1) * tile]
        return carry

    lax.fori_loop(0, n_col, body, 0)


def kept_partials(goff, moff, oidx, flow_flat, graph_flat, n_out, n_q, n_g):
    tile = flow_flat.shape[-1]
    kernel = functools.partial(column_kernel, n_q=n_q, n_g=n_g)
    return pl.pallas_call(
        kernel,
        out_shape=jax.ShapeDtypeStruct((n_out, tile, tile), jnp.float32),
        in_specs=[
            pl.BlockSpec(memory_space=pltpu.SMEM),
            pl.BlockSpec(memory_space=pltpu.SMEM),
            pl.BlockSpec(memory_space=pltpu.SMEM),
            pl.BlockSpec(memory_space=pltpu.VMEM),
            pl.BlockSpec(memory_space=pltpu.VMEM),
        ],
        out_specs=pl.BlockSpec(memory_space=pltpu.VMEM),
        scratch_shapes=[
            pltpu.VMEM((n_q * tile, n_g * tile), jnp.bfloat16),
            pltpu.VMEM((n_g * tile, tile), jnp.bfloat16),
        ],
        compiler_params=pltpu.CompilerParams(vmem_limit_bytes=48 * 1024 * 1024),
        cost_estimate=pl.CostEstimate(
            flops=2 * n_out * n_g * tile**3,
            transcendentals=0,
            bytes_accessed=2 * (flow_flat.size + graph_flat.size) + 4 * n_out * tile * tile,
        ),
    )(goff, moff, oidx, flow_flat, graph_flat)


def butterfly_sum(x, axis, n):
    d = 1
    while d < n:
        x = x + lax.ppermute(x, axis, [(i, i ^ d) for i in range(n)])
        d *= 2
    return x


def all_sum(x, axes, n):
    me = lax.axis_index(axes)
    parts = jnp.stack([x] + [lax.ppermute(x, axes, [(i, (i + s) % n) for i in range(n)]) for s in range(1, n)])
    total = parts[me % n]
    for src in range(1, n):
        total = total + parts[(me - src) % n]
    return total


def first_two(mask):
    n = mask.shape[-1]
    lo = jnp.argmax(mask, axis=-1).astype(jnp.int32)
    hi = (n - 1 - jnp.argmax(mask[..., ::-1], axis=-1)).astype(jnp.int32)
    return lo, hi


def local(a_tiles, a_coords, b_tiles, b_coords, out_coords):
    tile = a_tiles.shape[-1]
    rows_panel = a_tiles.shape[3]
    col_count = lax.axis_size("col")
    row_count = lax.axis_size("row")
    layer_count = lax.axis_size("layer")
    b_span = KA * col_count // row_count
    quarter = rows_panel // layer_count
    col_tiles = out_coords.shape[3]
    n_b = b_tiles.shape[3]
    my_row = lax.axis_index("row")

    own = b_tiles[0, 0, 0]
    far = lax.ppermute(own, "row", [(i, i ^ 2) for i in range(row_count)])
    near = lax.ppermute(own, "row", [(i, i ^ 1) for i in range(row_count)])
    far_near = lax.ppermute(far, "row", [(i, i ^ 1) for i in range(row_count)])
    graph_parts = [own, near, far, far_near]
    graph_tiles = jnp.concatenate(graph_parts, axis=0)
    graph_coords = lax.all_gather(b_coords[0, 0, 0][None], "row", axis=0, tiled=True)
    flow_tiles = lax.all_gather(a_tiles[0, 0, 0], "col", axis=0, tiled=True)
    flow_coords = lax.all_gather(a_coords[0, 0, 0][None], "col", axis=0, tiled=True)
    kept_all = lax.all_gather(out_coords[0, 0, 0][None], "layer", axis=0, tiled=True)

    n_out = layer_count * col_tiles
    col_ids = jnp.arange(col_tiles, dtype=jnp.int32)
    part_ids = jnp.arange(row_count, dtype=jnp.int32)
    owner_of_part = my_row ^ part_ids
    coords_by_part = graph_coords[owner_of_part]
    in_col = coords_by_part[:, None, :, 1] == col_ids[None, :, None]
    lo, hi = first_two(in_col)
    g_slot = jnp.stack([lo, hi], axis=2)
    g_b0 = jnp.take_along_axis(
        jnp.broadcast_to(coords_by_part[:, None, :, 0], in_col.shape), g_slot, axis=2
    )
    g_inner = owner_of_part[:, None, None] * b_span + g_b0
    goff = ((part_ids[:, None, None] * n_b + g_slot) * tile).transpose(1, 0, 2).reshape(col_tiles, -1)
    g_inner = g_inner.transpose(1, 0, 2).reshape(col_tiles, -1)
    n_g = goff.shape[1]

    kept_here = kept_all[:, None, :, 1] == col_ids[None, :, None]
    kept_pos = jnp.argmax(kept_here, axis=2).astype(jnp.int32)
    kept_row0 = jnp.take_along_axis(kept_all[:, :, 0], kept_pos, axis=1)
    q_ids = jnp.arange(layer_count, dtype=jnp.int32)
    kept_row = q_ids[:, None] * quarter + kept_row0
    oidx = (q_ids[:, None] * col_tiles + kept_pos).T

    a_rows = flow_coords[:, :, 0]
    a_inner = flow_coords[:, :, 1]
    grp = g_inner // KA
    want = g_inner % KA
    rows_q = kept_row.T
    slot_a = jnp.argmax(
        a_rows[grp[:, None, :], :] == rows_q[:, :, None, None], axis=3
    ).astype(jnp.int32)
    have = a_inner[grp[:, None, :], slot_a] == want[:, None, :]
    moff = jnp.where(have, (grp[:, None, :] * rows_panel + slot_a) * tile, -1)

    flow_flat = flow_tiles.reshape(-1, tile)
    graph_flat = graph_tiles.reshape(-1, tile)
    partial_sum = kept_partials(
        goff.reshape(-1).astype(jnp.int32),
        moff.reshape(-1).astype(jnp.int32),
        oidx.reshape(-1).astype(jnp.int32),
        flow_flat,
        graph_flat,
        n_out,
        layer_count,
        n_g,
    )
    kept_tiles = lax.psum_scatter(partial_sum, "layer", scatter_dimension=0, tiled=True)

    kept_cols = out_coords[0, 0, 0, :, 1]
    squared = kept_tiles * kept_tiles
    column_part = jnp.sum(squared, axis=1)
    local_mass = jnp.zeros_like(column_part).at[kept_cols].set(column_part)
    column_total = all_sum(local_mass, ("row", "layer"), row_count * layer_count)
    factor = jnp.float32(row_count * layer_count * tile) / column_total
    flow = squared * factor[kept_cols][:, None, :]
    return flow.reshape(1, 1, 1, col_tiles, tile, tile)


def solution(mesh):
    in_specs = (
        P("row", "col", "layer", None, None, None),
        P("row", "col", "layer", None, None),
        P("row", "col", "layer", None, None, None),
        P("row", "col", "layer", None, None),
        P("row", "col", "layer", None, None),
    )
    out_specs = P("row", "col", "layer", None, None, None)
    return jax.shard_map(local, mesh=mesh, in_specs=in_specs, out_specs=out_specs, check_vma=False)
```

```python
import functools

import jax
import jax.numpy as jnp
from jax import lax
from jax.experimental import pallas as pl
from jax.experimental.pallas import tpu as pltpu
from jax.sharding import PartitionSpec as P

KA = 4


def column_kernel(goff_ref, moff_ref, oidx_ref, flow_ref, graph_ref, out_ref, lhs_ref, rhs_ref, *, n_q, n_g):
    tile = out_ref.shape[-1]
    n_col = out_ref.shape[0] // n_q

    def body(j, carry):
        for g in range(n_g):
            g_off = pl.multiple_of(goff_ref[j * n_g + g], tile)
            rhs_ref[pl.ds(g * tile, tile), :] = graph_ref[pl.ds(g_off, tile), :]
        for q in range(n_q):
            for g in range(n_g):
                m_off = moff_ref[(j * n_q + q) * n_g + g]
                left = flow_ref[pl.ds(pl.multiple_of(jnp.maximum(m_off, 0), tile), tile), :]
                left = jnp.where(m_off >= 0, left, jnp.zeros_like(left))
                lhs_ref[pl.ds(q * tile, tile), pl.ds(g * tile, tile)] = left
        res = jnp.dot(lhs_ref[...], rhs_ref[...], preferred_element_type=jnp.float32)
        for q in range(n_q):
            out_ref[oidx_ref[j * n_q + q]] = res[q * tile : (q + 1) * tile]
        return carry

    lax.fori_loop(0, n_col, body, 0)


def kept_partials(goff, moff, oidx, flow_flat, graph_flat, n_out, n_q, n_g):
    tile = flow_flat.shape[-1]
    kernel = functools.partial(column_kernel, n_q=n_q, n_g=n_g)
    return pl.pallas_call(
        kernel,
        out_shape=jax.ShapeDtypeStruct((n_out, tile, tile), jnp.float32),
        in_specs=[
            pl.BlockSpec(memory_space=pltpu.SMEM),
            pl.BlockSpec(memory_space=pltpu.SMEM),
            pl.BlockSpec(memory_space=pltpu.SMEM),
            pl.BlockSpec(memory_space=pltpu.VMEM),
            pl.BlockSpec(memory_space=pltpu.VMEM),
        ],
        out_specs=pl.BlockSpec(memory_space=pltpu.VMEM),
        scratch_shapes=[
            pltpu.VMEM((n_q * tile, n_g * tile), jnp.bfloat16),
            pltpu.VMEM((n_g * tile, tile), jnp.bfloat16),
        ],
        compiler_params=pltpu.CompilerParams(vmem_limit_bytes=48 * 1024 * 1024),
        cost_estimate=pl.CostEstimate(
            flops=2 * n_out * n_g * tile**3,
            transcendentals=0,
            bytes_accessed=2 * (flow_flat.size + graph_flat.size) + 4 * n_out * tile * tile,
        ),
    )(goff, moff, oidx, flow_flat, graph_flat)


def butterfly_sum(x, axis, n):
    d = 1
    while d < n:
        x = x + lax.ppermute(x, axis, [(i, i ^ d) for i in range(n)])
        d *= 2
    return x


def first_two(mask):
    n = mask.shape[-1]
    lo = jnp.argmax(mask, axis=-1).astype(jnp.int32)
    hi = (n - 1 - jnp.argmax(mask[..., ::-1], axis=-1)).astype(jnp.int32)
    return lo, hi


def local(a_tiles, a_coords, b_tiles, b_coords, out_coords):
    tile = a_tiles.shape[-1]
    rows_panel = a_tiles.shape[3]
    col_count = lax.axis_size("col")
    row_count = lax.axis_size("row")
    layer_count = lax.axis_size("layer")
    b_span = KA * col_count // row_count
    quarter = rows_panel // layer_count
    col_tiles = out_coords.shape[3]
    n_b = b_tiles.shape[3]
    my_row = lax.axis_index("row")

    own = b_tiles[0, 0, 0]
    far = lax.ppermute(own, "row", [(i, i ^ 2) for i in range(row_count)])
    near = lax.ppermute(own, "row", [(i, i ^ 1) for i in range(row_count)])
    far_near = lax.ppermute(far, "row", [(i, i ^ 1) for i in range(row_count)])
    graph_parts = [own, near, far, far_near]
    graph_tiles = jnp.concatenate(graph_parts, axis=0)
    graph_coords = lax.all_gather(b_coords[0, 0, 0][None], "row", axis=0, tiled=True)
    flow_tiles = lax.all_gather(a_tiles[0, 0, 0], "col", axis=0, tiled=True)
    flow_coords = lax.all_gather(a_coords[0, 0, 0][None], "col", axis=0, tiled=True)
    kept_all = lax.all_gather(out_coords[0, 0, 0][None], "layer", axis=0, tiled=True)

    n_out = layer_count * col_tiles
    col_ids = jnp.arange(col_tiles, dtype=jnp.int32)
    part_ids = jnp.arange(row_count, dtype=jnp.int32)
    owner_of_part = my_row ^ part_ids
    coords_by_part = graph_coords[owner_of_part]
    in_col = coords_by_part[:, None, :, 1] == col_ids[None, :, None]
    lo, hi = first_two(in_col)
    g_slot = jnp.stack([lo, hi], axis=2)
    g_b0 = jnp.take_along_axis(
        jnp.broadcast_to(coords_by_part[:, None, :, 0], in_col.shape), g_slot, axis=2
    )
    g_inner = owner_of_part[:, None, None] * b_span + g_b0
    goff = ((part_ids[:, None, None] * n_b + g_slot) * tile).transpose(1, 0, 2).reshape(col_tiles, -1)
    g_inner = g_inner.transpose(1, 0, 2).reshape(col_tiles, -1)
    n_g = goff.shape[1]

    kept_here = kept_all[:, None, :, 1] == col_ids[None, :, None]
    kept_pos = jnp.argmax(kept_here, axis=2).astype(jnp.int32)
    kept_row0 = jnp.take_along_axis(kept_all[:, :, 0], kept_pos, axis=1)
    q_ids = jnp.arange(layer_count, dtype=jnp.int32)
    kept_row = q_ids[:, None] * quarter + kept_row0
    oidx = (q_ids[:, None] * col_tiles + kept_pos).T

    a_rows = flow_coords[:, :, 0]
    a_inner = flow_coords[:, :, 1]
    grp = g_inner // KA
    want = g_inner % KA
    rows_q = kept_row.T
    slot_a = jnp.argmax(
        a_rows[grp[:, None, :], :] == rows_q[:, :, None, None], axis=3
    ).astype(jnp.int32)
    have = a_inner[grp[:, None, :], slot_a] == want[:, None, :]
    moff = jnp.where(have, (grp[:, None, :] * rows_panel + slot_a) * tile, -1)

    flow_flat = flow_tiles.reshape(-1, tile)
    graph_flat = graph_tiles.reshape(-1, tile)
    partial_sum = kept_partials(
        goff.reshape(-1).astype(jnp.int32),
        moff.reshape(-1).astype(jnp.int32),
        oidx.reshape(-1).astype(jnp.int32),
        flow_flat,
        graph_flat,
        n_out,
        layer_count,
        n_g,
    )
    kept_tiles = lax.psum_scatter(partial_sum, "layer", scatter_dimension=0, tiled=True)

    kept_cols = out_coords[0, 0, 0, :, 1]
    squared = kept_tiles * kept_tiles
    column_part = jnp.sum(squared, axis=1)
    local_mass = jnp.zeros_like(column_part).at[kept_cols].set(column_part)
    column_total = butterfly_sum(butterfly_sum(local_mass, "row", row_count), "layer", layer_count)
    factor = jnp.float32(row_count * layer_count * tile) / column_total
    flow = squared * factor[kept_cols][:, None, :]
    return flow.reshape(1, 1, 1, col_tiles, tile, tile)


def solution(mesh):
    in_specs = (
        P("row", "col", "layer", None, None, None),
        P("row", "col", "layer", None, None),
        P("row", "col", "layer", None, None, None),
        P("row", "col", "layer", None, None),
        P("row", "col", "layer", None, None),
    )
    out_specs = P("row", "col", "layer", None, None, None)
    return jax.shard_map(local, mesh=mesh, in_specs=in_specs, out_specs=out_specs, check_vma=False)
```

```python
import functools

import jax
import jax.numpy as jnp
from jax import lax
from jax.experimental import pallas as pl
from jax.experimental.pallas import tpu as pltpu
from jax.sharding import PartitionSpec as P

KA = 4


def column_kernel(goff_ref, moff_ref, oidx_ref, flow_ref, graph_ref, out_ref, lhs_ref, rhs_ref, *, n_q, n_g):
    tile = out_ref.shape[-1]
    n_col = out_ref.shape[0] // n_q

    def body(j, carry):
        for g in range(n_g):
            g_off = pl.multiple_of(goff_ref[j * n_g + g], tile)
            rhs_ref[pl.ds(g * tile, tile), :] = graph_ref[pl.ds(g_off, tile), :]
        for q in range(n_q):
            for g in range(n_g):
                m_off = moff_ref[(j * n_q + q) * n_g + g]
                left = flow_ref[pl.ds(pl.multiple_of(jnp.maximum(m_off, 0), tile), tile), :]
                left = jnp.where(m_off >= 0, left, jnp.zeros_like(left))
                lhs_ref[pl.ds(q * tile, tile), pl.ds(g * tile, tile)] = left
        res = jnp.dot(lhs_ref[...], rhs_ref[...], preferred_element_type=jnp.float32)
        for q in range(n_q):
            out_ref[oidx_ref[j * n_q + q]] = res[q * tile : (q + 1) * tile]
        return carry

    lax.fori_loop(0, n_col, body, 0)


def kept_partials(goff, moff, oidx, flow_flat, graph_flat, n_out, n_q, n_g):
    tile = flow_flat.shape[-1]
    kernel = functools.partial(column_kernel, n_q=n_q, n_g=n_g)
    return pl.pallas_call(
        kernel,
        out_shape=jax.ShapeDtypeStruct((n_out, tile, tile), jnp.float32),
        in_specs=[
            pl.BlockSpec(memory_space=pltpu.SMEM),
            pl.BlockSpec(memory_space=pltpu.SMEM),
            pl.BlockSpec(memory_space=pltpu.SMEM),
            pl.BlockSpec(memory_space=pltpu.VMEM),
            pl.BlockSpec(memory_space=pltpu.VMEM),
        ],
        out_specs=pl.BlockSpec(memory_space=pltpu.VMEM),
        scratch_shapes=[
            pltpu.VMEM((n_q * tile, n_g * tile), jnp.bfloat16),
            pltpu.VMEM((n_g * tile, tile), jnp.bfloat16),
        ],
        compiler_params=pltpu.CompilerParams(vmem_limit_bytes=48 * 1024 * 1024),
        cost_estimate=pl.CostEstimate(
            flops=2 * n_out * n_g * tile**3,
            transcendentals=0,
            bytes_accessed=2 * (flow_flat.size + graph_flat.size) + 4 * n_out * tile * tile,
        ),
    )(goff, moff, oidx, flow_flat, graph_flat)


def butterfly_sum(x, axis, n):
    d = 1
    while d < n:
        x = x + lax.ppermute(x, axis, [(i, i ^ d) for i in range(n)])
        d *= 2
    return x


def first_two(mask):
    n = mask.shape[-1]
    lo = jnp.argmax(mask, axis=-1).astype(jnp.int32)
    hi = (n - 1 - jnp.argmax(mask[..., ::-1], axis=-1)).astype(jnp.int32)
    return lo, hi


def local(a_tiles, a_coords, b_tiles, b_coords, out_coords):
    tile = a_tiles.shape[-1]
    rows_panel = a_tiles.shape[3]
    col_count = lax.axis_size("col")
    row_count = lax.axis_size("row")
    layer_count = lax.axis_size("layer")
    b_span = KA * col_count // row_count
    quarter = rows_panel // layer_count
    col_tiles = out_coords.shape[3]
    n_b = b_tiles.shape[3]
    my_row = lax.axis_index("row")

    own = b_tiles[0, 0, 0]
    far = lax.ppermute(own, "row", [(i, i ^ 2) for i in range(row_count)])
    near = lax.ppermute(own, "row", [(i, i ^ 1) for i in range(row_count)])
    far_near = lax.ppermute(far, "row", [(i, i ^ 1) for i in range(row_count)])
    graph_parts = [own, near, far, far_near]
    graph_tiles = jnp.concatenate(graph_parts, axis=0)
    graph_coords = lax.all_gather(b_coords[0, 0, 0][None], "row", axis=0, tiled=True)
    flow_tiles = lax.all_gather(a_tiles[0, 0, 0], "col", axis=0, tiled=True)
    flow_coords = lax.all_gather(a_coords[0, 0, 0][None], "col", axis=0, tiled=True)
    kept_all = lax.all_gather(out_coords[0, 0, 0][None], "layer", axis=0, tiled=True)

    n_out = layer_count * col_tiles
    col_ids = jnp.arange(col_tiles, dtype=jnp.int32)
    part_ids = jnp.arange(row_count, dtype=jnp.int32)
    owner_of_part = my_row ^ part_ids
    coords_by_part = graph_coords[owner_of_part]
    in_col = coords_by_part[:, None, :, 1] == col_ids[None, :, None]
    lo, hi = first_two(in_col)
    g_slot = jnp.stack([lo, hi], axis=2)
    g_b0 = jnp.take_along_axis(
        jnp.broadcast_to(coords_by_part[:, None, :, 0], in_col.shape), g_slot, axis=2
    )
    g_inner = owner_of_part[:, None, None] * b_span + g_b0
    goff = ((part_ids[:, None, None] * n_b + g_slot) * tile).transpose(1, 0, 2).reshape(col_tiles, -1)
    g_inner = g_inner.transpose(1, 0, 2).reshape(col_tiles, -1)
    n_g = goff.shape[1]

    kept_here = kept_all[:, None, :, 1] == col_ids[None, :, None]
    kept_pos = jnp.argmax(kept_here, axis=2).astype(jnp.int32)
    kept_row0 = jnp.take_along_axis(kept_all[:, :, 0], kept_pos, axis=1)
    q_ids = jnp.arange(layer_count, dtype=jnp.int32)
    kept_row = q_ids[:, None] * quarter + kept_row0
    oidx = (q_ids[:, None] * col_tiles + kept_pos).T

    a_rows = flow_coords[:, :, 0]
    a_inner = flow_coords[:, :, 1]
    grp = g_inner // KA
    want = g_inner % KA
    rows_q = kept_row.T
    slot_a = jnp.argmax(
        a_rows[grp[:, None, :], :] == rows_q[:, :, None, None], axis=3
    ).astype(jnp.int32)
    have = a_inner[grp[:, None, :], slot_a] == want[:, None, :]
    moff = jnp.where(have, (grp[:, None, :] * rows_panel + slot_a) * tile, -1)

    flow_flat = flow_tiles.reshape(-1, tile)
    graph_flat = graph_tiles.reshape(-1, tile)
    partial_sum = kept_partials(
        goff.reshape(-1).astype(jnp.int32),
        moff.reshape(-1).astype(jnp.int32),
        oidx.reshape(-1).astype(jnp.int32),
        flow_flat,
        graph_flat,
        n_out,
        layer_count,
        n_g,
    )
    my_layer = lax.axis_index("layer")
    by_quarter = partial_sum.reshape(layer_count, col_tiles, tile, tile)
    kept_tiles = by_quarter[my_layer]
    for s in range(1, layer_count):
        send = by_quarter[(my_layer + s) % layer_count]
        kept_tiles = kept_tiles + lax.ppermute(
            send, "layer", [(i, (i + s) % layer_count) for i in range(layer_count)]
        )

    kept_cols = out_coords[0, 0, 0, :, 1]
    squared = kept_tiles * kept_tiles
    column_part = jnp.sum(squared, axis=1)
    local_mass = jnp.zeros_like(column_part).at[kept_cols].set(column_part)
    column_total = butterfly_sum(butterfly_sum(local_mass, "row", row_count), "layer", layer_count)
    factor = jnp.float32(row_count * layer_count * tile) / column_total
    flow = squared * factor[kept_cols][:, None, :]
    return flow.reshape(1, 1, 1, col_tiles, tile, tile)


def solution(mesh):
    in_specs = (
        P("row", "col", "layer", None, None, None),
        P("row", "col", "layer", None, None),
        P("row", "col", "layer", None, None, None),
        P("row", "col", "layer", None, None),
        P("row", "col", "layer", None, None),
    )
    out_specs = P("row", "col", "layer", None, None, None)
    return jax.shard_map(local, mesh=mesh, in_specs=in_specs, out_specs=out_specs, check_vma=False)
```

```python
import functools

import jax
import jax.numpy as jnp
from jax import lax
from jax.experimental import pallas as pl
from jax.experimental.pallas import tpu as pltpu
from jax.sharding import PartitionSpec as P

KA = 4
PAD = 16


def column_kernel(goff_ref, moff_ref, oidx_ref, flow_ref, graph_ref, out_ref, lhs_ref, rhs_ref, *, n_q, n_g):
    tile = out_ref.shape[-1]
    n_col = out_ref.shape[0] // n_q

    def body(j, carry):
        for g in range(n_g):
            g_off = pl.multiple_of(goff_ref[j * n_g + g], PAD)
            rhs_ref[pl.ds(g * tile, tile), :] = graph_ref[pl.ds(g_off, tile), :]
        for q in range(n_q):
            for g in range(n_g):
                m_off = moff_ref[(j * n_q + q) * n_g + g]
                left = flow_ref[pl.ds(pl.multiple_of(jnp.maximum(m_off, 0), PAD), tile), :]
                left = jnp.where(m_off >= 0, left, jnp.zeros_like(left))
                lhs_ref[pl.ds(q * tile, tile), pl.ds(g * tile, tile)] = left
        res = jnp.dot(lhs_ref[...], rhs_ref[...], preferred_element_type=jnp.float32)
        for q in range(n_q):
            out_ref[oidx_ref[j * n_q + q]] = res[q * tile : (q + 1) * tile]
        return carry

    lax.fori_loop(0, n_col, body, 0)


def kept_partials(goff, moff, oidx, flow_flat, graph_flat, n_out, n_q, n_g):
    tile = flow_flat.shape[-1]
    kernel = functools.partial(column_kernel, n_q=n_q, n_g=n_g)
    return pl.pallas_call(
        kernel,
        out_shape=jax.ShapeDtypeStruct((n_out, tile, tile), jnp.float32),
        in_specs=[
            pl.BlockSpec(memory_space=pltpu.SMEM),
            pl.BlockSpec(memory_space=pltpu.SMEM),
            pl.BlockSpec(memory_space=pltpu.SMEM),
            pl.BlockSpec(memory_space=pltpu.VMEM),
            pl.BlockSpec(memory_space=pltpu.VMEM),
        ],
        out_specs=pl.BlockSpec(memory_space=pltpu.VMEM),
        scratch_shapes=[
            pltpu.VMEM((n_q * tile, n_g * tile), jnp.bfloat16),
            pltpu.VMEM((n_g * tile, tile), jnp.bfloat16),
        ],
        compiler_params=pltpu.CompilerParams(vmem_limit_bytes=48 * 1024 * 1024),
        cost_estimate=pl.CostEstimate(
            flops=2 * n_out * n_g * tile**3,
            transcendentals=0,
            bytes_accessed=2 * (flow_flat.size + graph_flat.size) + 4 * n_out * tile * tile,
        ),
    )(goff, moff, oidx, flow_flat, graph_flat)


def butterfly_sum(x, axis, n):
    d = 1
    while d < n:
        x = x + lax.ppermute(x, axis, [(i, i ^ d) for i in range(n)])
        d *= 2
    return x


def pack_rows(tiles, rows):
    tile = tiles.shape[-1]
    extra = jnp.zeros((PAD, tile), jnp.bfloat16)
    extra = extra.at[: rows.shape[0], : rows.shape[1]].set(rows.astype(jnp.bfloat16))
    return jnp.concatenate([tiles.reshape(-1, tile), extra], axis=0)


def first_two(mask):
    n = mask.shape[-1]
    lo = jnp.argmax(mask, axis=-1).astype(jnp.int32)
    hi = (n - 1 - jnp.argmax(mask[..., ::-1], axis=-1)).astype(jnp.int32)
    return lo, hi


def local(a_tiles, a_coords, b_tiles, b_coords, out_coords):
    tile = a_tiles.shape[-1]
    rows_panel = a_tiles.shape[3]
    col_count = lax.axis_size("col")
    row_count = lax.axis_size("row")
    layer_count = lax.axis_size("layer")
    b_span = KA * col_count // row_count
    quarter = rows_panel // layer_count
    col_tiles = out_coords.shape[3]
    n_b = b_tiles.shape[3]
    my_row = lax.axis_index("row")
    my_layer = lax.axis_index("layer")

    own = pack_rows(b_tiles[0, 0, 0], b_coords[0, 0, 0].T)
    far = lax.ppermute(own, "row", [(i, i ^ 2) for i in range(row_count)])
    near = lax.ppermute(own, "row", [(i, i ^ 1) for i in range(row_count)])
    far_near = lax.ppermute(far, "row", [(i, i ^ 1) for i in range(row_count)])
    graph_parts = [own, near, far, far_near]
    g_stride = n_b * tile + PAD
    graph_flat = jnp.concatenate(graph_parts, axis=0)
    coords_by_part = jnp.stack(
        [p[n_b * tile : n_b * tile + 2, :n_b] for p in graph_parts]
    ).astype(jnp.int32).transpose(0, 2, 1)
    kept_parts = jnp.stack(
        [out_coords[0, 0, 0]]
        + [
            lax.ppermute(out_coords[0, 0, 0], "layer", [(i, (i + s) % layer_count) for i in range(layer_count)])
            for s in range(1, layer_count)
        ]
    )
    q_ids = jnp.arange(layer_count, dtype=jnp.int32)
    kept_all = kept_parts[(my_layer - q_ids) % layer_count]
    a_own = pack_rows(a_tiles[0, 0, 0], a_coords[0, 0, 0].T)
    a_stride = a_own.shape[0]
    flow_all = lax.all_to_all(
        jnp.broadcast_to(a_own[None], (col_count,) + a_own.shape), "col", 0, 0, tiled=True
    )
    flow_coords = flow_all[:, rows_panel * tile : rows_panel * tile + 2, :rows_panel].astype(jnp.int32)
    flow_coords = flow_coords.transpose(0, 2, 1)

    n_out = layer_count * col_tiles
    col_ids = jnp.arange(col_tiles, dtype=jnp.int32)
    part_ids = jnp.arange(row_count, dtype=jnp.int32)
    owner_of_part = my_row ^ part_ids
    in_col = coords_by_part[:, None, :, 1] == col_ids[None, :, None]
    lo, hi = first_two(in_col)
    g_slot = jnp.stack([lo, hi], axis=2)
    g_b0 = jnp.take_along_axis(
        jnp.broadcast_to(coords_by_part[:, None, :, 0], in_col.shape), g_slot, axis=2
    )
    g_inner = owner_of_part[:, None, None] * b_span + g_b0
    goff = (part_ids[:, None, None] * g_stride + g_slot * tile).transpose(1, 0, 2).reshape(col_tiles, -1)
    g_inner = g_inner.transpose(1, 0, 2).reshape(col_tiles, -1)
    n_g = goff.shape[1]

    kept_here = kept_all[:, None, :, 1] == col_ids[None, :, None]
    kept_pos = jnp.argmax(kept_here, axis=2).astype(jnp.int32)
    kept_row0 = jnp.take_along_axis(kept_all[:, :, 0], kept_pos, axis=1)
    q_ids = jnp.arange(layer_count, dtype=jnp.int32)
    kept_row = q_ids[:, None] * quarter + kept_row0
    oidx = (q_ids[:, None] * col_tiles + kept_pos).T

    a_rows = flow_coords[:, :, 0]
    a_inner = flow_coords[:, :, 1]
    grp = g_inner // KA
    want = g_inner % KA
    rows_q = kept_row.T
    slot_a = jnp.argmax(
        a_rows[grp[:, None, :], :] == rows_q[:, :, None, None], axis=3
    ).astype(jnp.int32)
    have = a_inner[grp[:, None, :], slot_a] == want[:, None, :]
    moff = jnp.where(have, grp[:, None, :] * a_stride + slot_a * tile, -1)

    flow_flat = flow_all.reshape(-1, tile)
    partial_sum = kept_partials(
        goff.reshape(-1).astype(jnp.int32),
        moff.reshape(-1).astype(jnp.int32),
        oidx.reshape(-1).astype(jnp.int32),
        flow_flat,
        graph_flat,
        n_out,
        layer_count,
        n_g,
    )
    kept_tiles = lax.psum_scatter(partial_sum, "layer", scatter_dimension=0, tiled=True)

    kept_cols = out_coords[0, 0, 0, :, 1]
    squared = kept_tiles * kept_tiles
    column_part = jnp.sum(squared, axis=1)
    local_mass = jnp.zeros_like(column_part).at[kept_cols].set(column_part)
    column_total = butterfly_sum(butterfly_sum(local_mass, "row", row_count), "layer", layer_count)
    factor = jnp.float32(row_count * layer_count * tile) / column_total
    flow = squared * factor[kept_cols][:, None, :]
    return flow.reshape(1, 1, 1, col_tiles, tile, tile)


def solution(mesh):
    in_specs = (
        P("row", "col", "layer", None, None, None),
        P("row", "col", "layer", None, None),
        P("row", "col", "layer", None, None, None),
        P("row", "col", "layer", None, None),
        P("row", "col", "layer", None, None),
    )
    out_specs = P("row", "col", "layer", None, None, None)
    return jax.shard_map(local, mesh=mesh, in_specs=in_specs, out_specs=out_specs, check_vma=False)
```

```python
import functools

import jax
import jax.numpy as jnp
from jax import lax
from jax.experimental import pallas as pl
from jax.experimental.pallas import tpu as pltpu
from jax.sharding import PartitionSpec as P

KA = 4


def column_kernel(goff_ref, moff_ref, oidx_ref, flow_ref, graph_ref, out_ref, lhs_ref, rhs_ref, *, n_q, n_g):
    tile = out_ref.shape[-1]
    n_col = out_ref.shape[0] // n_q

    def body(j, carry):
        for g in range(n_g):
            g_off = pl.multiple_of(goff_ref[j * n_g + g], tile)
            rhs_ref[pl.ds(g * tile, tile), :] = graph_ref[pl.ds(g_off, tile), :]
        for q in range(n_q):
            for g in range(n_g):
                m_off = moff_ref[(j * n_q + q) * n_g + g]
                left = flow_ref[pl.ds(pl.multiple_of(jnp.maximum(m_off, 0), tile), tile), :]
                left = jnp.where(m_off >= 0, left, jnp.zeros_like(left))
                lhs_ref[pl.ds(q * tile, tile), pl.ds(g * tile, tile)] = left
        res = jnp.dot(lhs_ref[...], rhs_ref[...], preferred_element_type=jnp.float32)
        for q in range(n_q):
            out_ref[oidx_ref[j * n_q + q]] = res[q * tile : (q + 1) * tile]
        return carry

    lax.fori_loop(0, n_col, body, 0)


def kept_partials(goff, moff, oidx, flow_flat, graph_flat, n_out, n_q, n_g):
    tile = flow_flat.shape[-1]
    kernel = functools.partial(column_kernel, n_q=n_q, n_g=n_g)
    return pl.pallas_call(
        kernel,
        out_shape=jax.ShapeDtypeStruct((n_out, tile, tile), jnp.float32),
        in_specs=[
            pl.BlockSpec(memory_space=pltpu.SMEM),
            pl.BlockSpec(memory_space=pltpu.SMEM),
            pl.BlockSpec(memory_space=pltpu.SMEM),
            pl.BlockSpec(memory_space=pltpu.VMEM),
            pl.BlockSpec(memory_space=pltpu.VMEM),
        ],
        out_specs=pl.BlockSpec(memory_space=pltpu.VMEM),
        scratch_shapes=[
            pltpu.VMEM((n_q * tile, n_g * tile), jnp.bfloat16),
            pltpu.VMEM((n_g * tile, tile), jnp.bfloat16),
        ],
        compiler_params=pltpu.CompilerParams(vmem_limit_bytes=48 * 1024 * 1024),
        cost_estimate=pl.CostEstimate(
            flops=2 * n_out * n_g * tile**3,
            transcendentals=0,
            bytes_accessed=2 * (flow_flat.size + graph_flat.size) + 4 * n_out * tile * tile,
        ),
    )(goff, moff, oidx, flow_flat, graph_flat)


def butterfly_sum(x, axis, n):
    d = 1
    while d < n:
        x = x + lax.ppermute(x, axis, [(i, i ^ d) for i in range(n)])
        d *= 2
    return x


def first_two(mask):
    n = mask.shape[-1]
    lo = jnp.argmax(mask, axis=-1).astype(jnp.int32)
    hi = (n - 1 - jnp.argmax(mask[..., ::-1], axis=-1)).astype(jnp.int32)
    return lo, hi


def local(a_tiles, a_coords, b_tiles, b_coords, out_coords):
    tile = a_tiles.shape[-1]
    rows_panel = a_tiles.shape[3]
    col_count = lax.axis_size("col")
    row_count = lax.axis_size("row")
    layer_count = lax.axis_size("layer")
    b_span = KA * col_count // row_count
    quarter = rows_panel // layer_count
    col_tiles = out_coords.shape[3]
    n_b = b_tiles.shape[3]
    my_row = lax.axis_index("row")

    own = b_tiles[0, 0, 0]
    far = lax.ppermute(own, "row", [(i, i ^ 2) for i in range(row_count)])
    near = lax.ppermute(own, "row", [(i, i ^ 1) for i in range(row_count)])
    far_near = lax.ppermute(far, "row", [(i, i ^ 1) for i in range(row_count)])
    graph_parts = [own, near, far, far_near]
    graph_tiles = jnp.concatenate(graph_parts, axis=0)
    graph_coords = lax.all_gather(b_coords[0, 0, 0][None], "row", axis=0, tiled=True)
    flow_tiles = lax.all_gather(a_tiles[0, 0, 0], "col", axis=0, tiled=True)
    flow_coords = lax.all_gather(a_coords[0, 0, 0][None], "col", axis=0, tiled=True)
    kept_all = lax.all_gather(out_coords[0, 0, 0][None], "layer", axis=0, tiled=True)

    n_out = layer_count * col_tiles
    col_ids = jnp.arange(col_tiles, dtype=jnp.int32)
    part_ids = jnp.arange(row_count, dtype=jnp.int32)
    owner_of_part = my_row ^ part_ids
    coords_by_part = graph_coords[owner_of_part]
    in_col = coords_by_part[:, None, :, 1] == col_ids[None, :, None]
    lo, hi = first_two(in_col)
    g_slot = jnp.stack([lo, hi], axis=2)
    g_b0 = jnp.take_along_axis(
        jnp.broadcast_to(coords_by_part[:, None, :, 0], in_col.shape), g_slot, axis=2
    )
    g_inner = owner_of_part[:, None, None] * b_span + g_b0
    goff = ((part_ids[:, None, None] * n_b + g_slot) * tile).transpose(1, 0, 2).reshape(col_tiles, -1)
    g_inner = g_inner.transpose(1, 0, 2).reshape(col_tiles, -1)
    n_g = goff.shape[1]

    kept_here = kept_all[:, None, :, 1] == col_ids[None, :, None]
    kept_pos = jnp.argmax(kept_here, axis=2).astype(jnp.int32)
    kept_row0 = jnp.take_along_axis(kept_all[:, :, 0], kept_pos, axis=1)
    q_ids = jnp.arange(layer_count, dtype=jnp.int32)
    kept_row = q_ids[:, None] * quarter + kept_row0
    oidx = (q_ids[:, None] * col_tiles + kept_pos).T

    a_rows = flow_coords[:, :, 0]
    a_inner = flow_coords[:, :, 1]
    grp = g_inner // KA
    want = g_inner % KA
    rows_q = kept_row.T
    slot_a = jnp.argmax(
        a_rows[grp[:, None, :], :] == rows_q[:, :, None, None], axis=3
    ).astype(jnp.int32)
    have = a_inner[grp[:, None, :], slot_a] == want[:, None, :]
    moff = jnp.where(have, (grp[:, None, :] * rows_panel + slot_a) * tile, -1)

    flow_flat = flow_tiles.reshape(-1, tile)
    graph_flat = graph_tiles.reshape(-1, tile)
    partial_sum = kept_partials(
        goff.reshape(-1).astype(jnp.int32),
        moff.reshape(-1).astype(jnp.int32),
        oidx.reshape(-1).astype(jnp.int32),
        flow_flat,
        graph_flat,
        n_out,
        layer_count,
        n_g,
    )
    from_layers = lax.all_to_all(
        partial_sum.reshape(layer_count, col_tiles, tile, tile), "layer", 0, 0, tiled=True
    )
    kept_tiles = jnp.sum(from_layers, axis=0)

    kept_cols = out_coords[0, 0, 0, :, 1]
    squared = kept_tiles * kept_tiles
    column_part = jnp.sum(squared, axis=1)
    local_mass = jnp.zeros_like(column_part).at[kept_cols].set(column_part)
    column_total = butterfly_sum(butterfly_sum(local_mass, "row", row_count), "layer", layer_count)
    factor = jnp.float32(row_count * layer_count * tile) / column_total
    flow = squared * factor[kept_cols][:, None, :]
    return flow.reshape(1, 1, 1, col_tiles, tile, tile)


def solution(mesh):
    in_specs = (
        P("row", "col", "layer", None, None, None),
        P("row", "col", "layer", None, None),
        P("row", "col", "layer", None, None, None),
        P("row", "col", "layer", None, None),
        P("row", "col", "layer", None, None),
    )
    out_specs = P("row", "col", "layer", None, None, None)
    return jax.shard_map(local, mesh=mesh, in_specs=in_specs, out_specs=out_specs, check_vma=False)
```

```python
import functools

import jax
import jax.numpy as jnp
from jax import lax
from jax.experimental import pallas as pl
from jax.experimental.pallas import tpu as pltpu
from jax.sharding import PartitionSpec as P

KA = 4


def column_kernel(moff_ref, oidx_ref, flow_ref, graph_ref, out_ref, lhs_ref, *, n_q, n_g):
    tile = out_ref.shape[-1]
    n_col = out_ref.shape[0] // n_q

    def body(j, carry):
        for q in range(n_q):
            for g in range(n_g):
                m_off = moff_ref[(j * n_q + q) * n_g + g]
                left = flow_ref[pl.ds(pl.multiple_of(jnp.maximum(m_off, 0), tile), tile), :]
                left = jnp.where(m_off >= 0, left, jnp.zeros_like(left))
                lhs_ref[pl.ds(q * tile, tile), pl.ds(g * tile, tile)] = left
        right = graph_ref[pl.ds(pl.multiple_of(j * n_g * tile, n_g * tile), n_g * tile), :]
        res = jnp.dot(lhs_ref[...], right, preferred_element_type=jnp.float32)
        for q in range(n_q):
            out_ref[oidx_ref[j * n_q + q]] = res[q * tile : (q + 1) * tile]
        return carry

    lax.fori_loop(0, n_col, body, 0)


def kept_partials(moff, oidx, flow_flat, graph_flat, n_out, n_q, n_g):
    tile = flow_flat.shape[-1]
    kernel = functools.partial(column_kernel, n_q=n_q, n_g=n_g)
    return pl.pallas_call(
        kernel,
        out_shape=jax.ShapeDtypeStruct((n_out, tile, tile), jnp.float32),
        in_specs=[
            pl.BlockSpec(memory_space=pltpu.SMEM),
            pl.BlockSpec(memory_space=pltpu.SMEM),
            pl.BlockSpec(memory_space=pltpu.VMEM),
            pl.BlockSpec(memory_space=pltpu.VMEM),
        ],
        out_specs=pl.BlockSpec(memory_space=pltpu.VMEM),
        scratch_shapes=[
            pltpu.VMEM((n_q * tile, n_g * tile), jnp.bfloat16),
        ],
        compiler_params=pltpu.CompilerParams(vmem_limit_bytes=48 * 1024 * 1024),
        cost_estimate=pl.CostEstimate(
            flops=2 * n_out * n_g * tile**3,
            transcendentals=0,
            bytes_accessed=2 * (flow_flat.size + graph_flat.size) + 4 * n_out * tile * tile,
        ),
    )(moff, oidx, flow_flat, graph_flat)


def butterfly_sum(x, axis, n, masks):
    for d in masks:
        x = x + lax.ppermute(x, axis, [(i, i ^ d) for i in range(n)])
    return x


def first_two(mask):
    n = mask.shape[-1]
    lo = jnp.argmax(mask, axis=-1).astype(jnp.int32)
    hi = (n - 1 - jnp.argmax(mask[..., ::-1], axis=-1)).astype(jnp.int32)
    return lo, hi


def local(a_tiles, a_coords, b_tiles, b_coords, out_coords):
    tile = a_tiles.shape[-1]
    rows_panel = a_tiles.shape[3]
    col_count = lax.axis_size("col")
    row_count = lax.axis_size("row")
    layer_count = lax.axis_size("layer")
    b_span = KA * col_count // row_count
    quarter = rows_panel // layer_count
    col_tiles = out_coords.shape[3]
    n_b = b_tiles.shape[3]
    my_row = lax.axis_index("row")

    own = b_tiles[0, 0, 0]
    far = lax.ppermute(own, "row", [(i, i ^ 2) for i in range(row_count)])
    near = lax.ppermute(own, "row", [(i, i ^ 1) for i in range(row_count)])
    far_near = lax.ppermute(far, "row", [(i, i ^ 1) for i in range(row_count)])
    graph_parts = [own, near, far, far_near]
    graph_tiles = jnp.concatenate(graph_parts, axis=0)
    graph_coords = lax.all_gather(b_coords[0, 0, 0][None], "row", axis=0, tiled=True)
    flow_tiles = lax.all_gather(a_tiles[0, 0, 0], "col", axis=0, tiled=True)
    flow_coords = lax.all_gather(a_coords[0, 0, 0][None], "col", axis=0, tiled=True)
    kept_all = lax.all_gather(out_coords[0, 0, 0][None], "layer", axis=0, tiled=True)

    n_out = layer_count * col_tiles
    col_ids = jnp.arange(col_tiles, dtype=jnp.int32)
    part_ids = jnp.arange(row_count, dtype=jnp.int32)
    owner_of_part = my_row ^ part_ids
    coords_by_part = graph_coords[owner_of_part]
    in_col = coords_by_part[:, None, :, 1] == col_ids[None, :, None]
    lo, hi = first_two(in_col)
    g_slot = jnp.stack([lo, hi], axis=2)
    g_b0 = jnp.take_along_axis(
        jnp.broadcast_to(coords_by_part[:, None, :, 0], in_col.shape), g_slot, axis=2
    )
    g_inner = owner_of_part[:, None, None] * b_span + g_b0
    g_tile = (part_ids[:, None, None] * n_b + g_slot).transpose(1, 0, 2).reshape(col_tiles, -1)
    g_inner = g_inner.transpose(1, 0, 2).reshape(col_tiles, -1)
    n_g = g_tile.shape[1]

    kept_here = kept_all[:, None, :, 1] == col_ids[None, :, None]
    kept_pos = jnp.argmax(kept_here, axis=2).astype(jnp.int32)
    kept_row0 = jnp.take_along_axis(kept_all[:, :, 0], kept_pos, axis=1)
    q_ids = jnp.arange(layer_count, dtype=jnp.int32)
    kept_row = q_ids[:, None] * quarter + kept_row0
    oidx = (q_ids[:, None] * col_tiles + kept_pos).T

    a_rows = flow_coords[:, :, 0]
    a_inner = flow_coords[:, :, 1]
    grp = g_inner // KA
    want = g_inner % KA
    rows_q = kept_row.T
    slot_a = jnp.argmax(
        a_rows[grp[:, None, :], :] == rows_q[:, :, None, None], axis=3
    ).astype(jnp.int32)
    have = a_inner[grp[:, None, :], slot_a] == want[:, None, :]
    moff = jnp.where(have, (grp[:, None, :] * rows_panel + slot_a) * tile, -1)

    flow_flat = flow_tiles.reshape(-1, tile)
    graph_flat = graph_tiles[g_tile.reshape(-1)].reshape(-1, tile)
    partial_sum = kept_partials(
        moff.reshape(-1).astype(jnp.int32),
        oidx.reshape(-1).astype(jnp.int32),
        flow_flat,
        graph_flat,
        n_out,
        layer_count,
        n_g,
    )
    kept_tiles = lax.psum_scatter(partial_sum, "layer", scatter_dimension=0, tiled=True)

    kept_cols = out_coords[0, 0, 0, :, 1]
    squared = kept_tiles * kept_tiles
    column_part = jnp.sum(squared, axis=1)
    local_mass = jnp.zeros_like(column_part).at[kept_cols].set(column_part)
    column_total = butterfly_sum(
        butterfly_sum(local_mass, "row", row_count, (1, 2)), "layer", layer_count, (1, 3)
    )
    factor = jnp.float32(row_count * layer_count * tile) / column_total
    flow = squared * factor[kept_cols][:, None, :]
    return flow.reshape(1, 1, 1, col_tiles, tile, tile)


def solution(mesh):
    in_specs = (
        P("row", "col", "layer", None, None, None),
        P("row", "col", "layer", None, None),
        P("row", "col", "layer", None, None, None),
        P("row", "col", "layer", None, None),
        P("row", "col", "layer", None, None),
    )
    out_specs = P("row", "col", "layer", None, None, None)
    return jax.shard_map(local, mesh=mesh, in_specs=in_specs, out_specs=out_specs, check_vma=False)
```

```python
import functools

import jax
import jax.numpy as jnp
from jax import lax
from jax.experimental import pallas as pl
from jax.experimental.pallas import tpu as pltpu
from jax.sharding import PartitionSpec as P

KA = 4


def column_kernel(moff_ref, oidx_ref, flow_hbm, graph_hbm, out_ref, lhs_ref, rhs_ref, lhs_sem, rhs_sem, *, n_q, n_g):
    tile = out_ref.shape[-1]
    n_col = out_ref.shape[0] // n_q
    span = n_g * tile

    def rhs_copy(j, slot):
        src = graph_hbm.at[pl.ds(pl.multiple_of(j * span, span), span), :]
        return pltpu.make_async_copy(src, rhs_ref.at[slot], rhs_sem.at[slot])

    def lhs_copy(j, slot, q, g):
        m_off = moff_ref[(j * n_q + q) * n_g + g]
        src = flow_hbm.at[pl.ds(pl.multiple_of(jnp.maximum(m_off, 0), tile), tile), :]
        dst = lhs_ref.at[slot, pl.ds(q * tile, tile), pl.ds(g * tile, tile)]
        return m_off, pltpu.make_async_copy(src, dst, lhs_sem.at[slot, q * n_g + g])

    def fetch(j, slot):
        rhs_copy(j, slot).start()
        for q in range(n_q):
            for g in range(n_g):
                m_off, copy = lhs_copy(j, slot, q, g)

                @pl.when(m_off >= 0)
                def _():
                    copy.start()

                @pl.when(m_off < 0)
                def _():
                    lhs_ref[slot, pl.ds(q * tile, tile), pl.ds(g * tile, tile)] = jnp.zeros(
                        (tile, tile), lhs_ref.dtype
                    )

    def wait(j, slot):
        rhs_copy(j, slot).wait()
        for q in range(n_q):
            for g in range(n_g):
                m_off, copy = lhs_copy(j, slot, q, g)

                @pl.when(m_off >= 0)
                def _():
                    copy.wait()

    fetch(0, 0)

    def body(j, carry):
        slot = j % 2

        @pl.when(j + 1 < n_col)
        def _():
            fetch(j + 1, 1 - slot)

        wait(j, slot)
        res = jnp.dot(lhs_ref[slot], rhs_ref[slot], preferred_element_type=jnp.float32)
        for q in range(n_q):
            out_ref[oidx_ref[j * n_q + q]] = res[q * tile : (q + 1) * tile]
        return carry

    lax.fori_loop(0, n_col, body, 0)


def kept_partials(moff, oidx, flow_flat, graph_flat, n_out, n_q, n_g):
    tile = flow_flat.shape[-1]
    kernel = functools.partial(column_kernel, n_q=n_q, n_g=n_g)
    return pl.pallas_call(
        kernel,
        out_shape=jax.ShapeDtypeStruct((n_out, tile, tile), jnp.float32),
        in_specs=[
            pl.BlockSpec(memory_space=pltpu.SMEM),
            pl.BlockSpec(memory_space=pltpu.SMEM),
            pl.BlockSpec(memory_space=pl.ANY),
            pl.BlockSpec(memory_space=pl.ANY),
        ],
        out_specs=pl.BlockSpec(memory_space=pltpu.VMEM),
        scratch_shapes=[
            pltpu.VMEM((2, n_q * tile, n_g * tile), jnp.bfloat16),
            pltpu.VMEM((2, n_g * tile, tile), jnp.bfloat16),
            pltpu.SemaphoreType.DMA((2, n_q * n_g)),
            pltpu.SemaphoreType.DMA((2,)),
        ],
        compiler_params=pltpu.CompilerParams(vmem_limit_bytes=48 * 1024 * 1024),
        cost_estimate=pl.CostEstimate(
            flops=2 * n_out * n_g * tile**3,
            transcendentals=0,
            bytes_accessed=2 * (flow_flat.size + graph_flat.size) + 4 * n_out * tile * tile,
        ),
    )(moff, oidx, flow_flat, graph_flat)


def butterfly_sum(x, axis, n, masks):
    for d in masks:
        x = x + lax.ppermute(x, axis, [(i, i ^ d) for i in range(n)])
    return x


def first_two(mask):
    n = mask.shape[-1]
    lo = jnp.argmax(mask, axis=-1).astype(jnp.int32)
    hi = (n - 1 - jnp.argmax(mask[..., ::-1], axis=-1)).astype(jnp.int32)
    return lo, hi


def local(a_tiles, a_coords, b_tiles, b_coords, out_coords):
    tile = a_tiles.shape[-1]
    rows_panel = a_tiles.shape[3]
    col_count = lax.axis_size("col")
    row_count = lax.axis_size("row")
    layer_count = lax.axis_size("layer")
    b_span = KA * col_count // row_count
    quarter = rows_panel // layer_count
    col_tiles = out_coords.shape[3]
    n_b = b_tiles.shape[3]
    my_row = lax.axis_index("row")

    own = b_tiles[0, 0, 0]
    far = lax.ppermute(own, "row", [(i, i ^ 2) for i in range(row_count)])
    near = lax.ppermute(own, "row", [(i, i ^ 1) for i in range(row_count)])
    far_near = lax.ppermute(far, "row", [(i, i ^ 1) for i in range(row_count)])
    graph_parts = [own, near, far, far_near]
    graph_tiles = jnp.concatenate(graph_parts, axis=0)
    graph_coords = lax.all_gather(b_coords[0, 0, 0][None], "row", axis=0, tiled=True)
    flow_tiles = lax.all_gather(a_tiles[0, 0, 0], "col", axis=0, tiled=True)
    flow_coords = lax.all_gather(a_coords[0, 0, 0][None], "col", axis=0, tiled=True)
    kept_all = lax.all_gather(out_coords[0, 0, 0][None], "layer", axis=0, tiled=True)

    n_out = layer_count * col_tiles
    col_ids = jnp.arange(col_tiles, dtype=jnp.int32)
    part_ids = jnp.arange(row_count, dtype=jnp.int32)
    owner_of_part = my_row ^ part_ids
    coords_by_part = graph_coords[owner_of_part]
    in_col = coords_by_part[:, None, :, 1] == col_ids[None, :, None]
    lo, hi = first_two(in_col)
    g_slot = jnp.stack([lo, hi], axis=2)
    g_b0 = jnp.take_along_axis(
        jnp.broadcast_to(coords_by_part[:, None, :, 0], in_col.shape), g_slot, axis=2
    )
    g_inner = owner_of_part[:, None, None] * b_span + g_b0
    g_tile = (part_ids[:, None, None] * n_b + g_slot).transpose(1, 0, 2).reshape(col_tiles, -1)
    g_inner = g_inner.transpose(1, 0, 2).reshape(col_tiles, -1)
    n_g = g_tile.shape[1]

    kept_here = kept_all[:, None, :, 1] == col_ids[None, :, None]
    kept_pos = jnp.argmax(kept_here, axis=2).astype(jnp.int32)
    kept_row0 = jnp.take_along_axis(kept_all[:, :, 0], kept_pos, axis=1)
    q_ids = jnp.arange(layer_count, dtype=jnp.int32)
    kept_row = q_ids[:, None] * quarter + kept_row0
    oidx = (q_ids[:, None] * col_tiles + kept_pos).T

    a_rows = flow_coords[:, :, 0]
    a_inner = flow_coords[:, :, 1]
    grp = g_inner // KA
    want = g_inner % KA
    rows_q = kept_row.T
    slot_a = jnp.argmax(
        a_rows[grp[:, None, :], :] == rows_q[:, :, None, None], axis=3
    ).astype(jnp.int32)
    have = a_inner[grp[:, None, :], slot_a] == want[:, None, :]
    moff = jnp.where(have, (grp[:, None, :] * rows_panel + slot_a) * tile, -1)

    flow_flat = flow_tiles.reshape(-1, tile)
    graph_flat = graph_tiles[g_tile.reshape(-1)].reshape(-1, tile)
    partial_sum = kept_partials(
        moff.reshape(-1).astype(jnp.int32),
        oidx.reshape(-1).astype(jnp.int32),
        flow_flat,
        graph_flat,
        n_out,
        layer_count,
        n_g,
    )
    kept_tiles = lax.psum_scatter(partial_sum, "layer", scatter_dimension=0, tiled=True)

    kept_cols = out_coords[0, 0, 0, :, 1]
    squared = kept_tiles * kept_tiles
    column_part = jnp.sum(squared, axis=1)
    local_mass = jnp.zeros_like(column_part).at[kept_cols].set(column_part)
    column_total = butterfly_sum(
        butterfly_sum(local_mass, "row", row_count, (1, 2)), "layer", layer_count, (1, 3)
    )
    factor = jnp.float32(row_count * layer_count * tile) / column_total
    flow = squared * factor[kept_cols][:, None, :]
    return flow.reshape(1, 1, 1, col_tiles, tile, tile)


def solution(mesh):
    in_specs = (
        P("row", "col", "layer", None, None, None),
        P("row", "col", "layer", None, None),
        P("row", "col", "layer", None, None, None),
        P("row", "col", "layer", None, None),
        P("row", "col", "layer", None, None),
    )
    out_specs = P("row", "col", "layer", None, None, None)
    return jax.shard_map(local, mesh=mesh, in_specs=in_specs, out_specs=out_specs, check_vma=False)
```

```python
import functools

import jax
import jax.numpy as jnp
from jax import lax
from jax.experimental import pallas as pl
from jax.experimental.pallas import tpu as pltpu
from jax.sharding import PartitionSpec as P

KA = 4


def column_kernel(moff_ref, oidx_ref, flow_ref, graph_ref, out_ref, lhs_ref, *, n_q, n_g):
    tile = out_ref.shape[-1]
    n_col = out_ref.shape[0] // n_q

    def body(j, carry):
        for q in range(n_q):
            for g in range(n_g):
                m_off = moff_ref[(j * n_q + q) * n_g + g]
                left = flow_ref[pl.ds(pl.multiple_of(jnp.maximum(m_off, 0), tile), tile), :]
                left = jnp.where(m_off >= 0, left, jnp.zeros_like(left))
                lhs_ref[pl.ds(q * tile, tile), pl.ds(g * tile, tile)] = left
        right = graph_ref[pl.ds(pl.multiple_of(j * n_g * tile, n_g * tile), n_g * tile), :]
        res = jnp.dot(lhs_ref[...], right, preferred_element_type=jnp.float32)
        for q in range(n_q):
            out_ref[oidx_ref[j * n_q + q]] = res[q * tile : (q + 1) * tile]
        return carry

    lax.fori_loop(0, n_col, body, 0)


def kept_partials(moff, oidx, flow_flat, graph_flat, n_out, n_q, n_g):
    tile = flow_flat.shape[-1]
    kernel = functools.partial(column_kernel, n_q=n_q, n_g=n_g)
    return pl.pallas_call(
        kernel,
        out_shape=jax.ShapeDtypeStruct((n_out, tile, tile), jnp.float32),
        in_specs=[
            pl.BlockSpec(memory_space=pltpu.SMEM),
            pl.BlockSpec(memory_space=pltpu.SMEM),
            pl.BlockSpec(memory_space=pltpu.VMEM),
            pl.BlockSpec(memory_space=pltpu.VMEM),
        ],
        out_specs=pl.BlockSpec(memory_space=pltpu.VMEM),
        scratch_shapes=[
            pltpu.VMEM((n_q * tile, n_g * tile), jnp.bfloat16),
        ],
        compiler_params=pltpu.CompilerParams(vmem_limit_bytes=48 * 1024 * 1024),
        cost_estimate=pl.CostEstimate(
            flops=2 * n_out * n_g * tile**3,
            transcendentals=0,
            bytes_accessed=2 * (flow_flat.size + graph_flat.size) + 4 * n_out * tile * tile,
        ),
    )(moff, oidx, flow_flat, graph_flat)


def butterfly_sum(x, axis, n, masks):
    for d in masks:
        x = x + lax.ppermute(x, axis, [(i, i ^ d) for i in range(n)])
    return x


def first_two(mask):
    n = mask.shape[-1]
    lo = jnp.argmax(mask, axis=-1).astype(jnp.int32)
    hi = (n - 1 - jnp.argmax(mask[..., ::-1], axis=-1)).astype(jnp.int32)
    return lo, hi


def local(a_tiles, a_coords, b_tiles, b_coords, out_coords):
    tile = a_tiles.shape[-1]
    rows_panel = a_tiles.shape[3]
    col_count = lax.axis_size("col")
    row_count = lax.axis_size("row")
    layer_count = lax.axis_size("layer")
    b_span = KA * col_count // row_count
    quarter = rows_panel // layer_count
    col_tiles = out_coords.shape[3]
    n_b = b_tiles.shape[3]
    my_row = lax.axis_index("row")

    own = b_tiles[0, 0, 0]
    far = lax.ppermute(own, "row", [(i, i ^ 2) for i in range(row_count)])
    near = lax.ppermute(own, "row", [(i, i ^ 1) for i in range(row_count)])
    far_near = lax.ppermute(far, "row", [(i, i ^ 1) for i in range(row_count)])
    graph_parts = [own, near, far, far_near]
    graph_tiles = jnp.concatenate(graph_parts, axis=0)
    graph_coords = lax.all_gather(b_coords[0, 0, 0][None], "row", axis=0, tiled=True)
    flow_tiles = lax.all_gather(a_tiles[0, 0, 0], "col", axis=0, tiled=True)
    flow_coords = lax.all_gather(a_coords[0, 0, 0][None], "col", axis=0, tiled=True)
    kept_all = lax.all_gather(out_coords[0, 0, 0][None], "layer", axis=0, tiled=True)

    n_out = layer_count * col_tiles
    col_ids = jnp.arange(col_tiles, dtype=jnp.int32)
    part_ids = jnp.arange(row_count, dtype=jnp.int32)
    owner_of_part = my_row ^ part_ids
    coords_by_part = graph_coords[owner_of_part]
    in_col = coords_by_part[:, None, :, 1] == col_ids[None, :, None]
    lo, hi = first_two(in_col)
    g_slot = jnp.stack([lo, hi], axis=2)
    g_b0 = jnp.take_along_axis(
        jnp.broadcast_to(coords_by_part[:, None, :, 0], in_col.shape), g_slot, axis=2
    )
    g_inner = owner_of_part[:, None, None] * b_span + g_b0
    g_tile = (part_ids[:, None, None] * n_b + g_slot).transpose(1, 0, 2).reshape(col_tiles, -1)
    g_inner = g_inner.transpose(1, 0, 2).reshape(col_tiles, -1)
    n_g = g_tile.shape[1]

    kept_here = kept_all[:, None, :, 1] == col_ids[None, :, None]
    kept_pos = jnp.argmax(kept_here, axis=2).astype(jnp.int32)
    kept_row0 = jnp.take_along_axis(kept_all[:, :, 0], kept_pos, axis=1)
    q_ids = jnp.arange(layer_count, dtype=jnp.int32)
    kept_row = q_ids[:, None] * quarter + kept_row0
    oidx = jnp.broadcast_to(q_ids[:, None] * col_tiles + col_ids[None, :], (layer_count, col_tiles)).T

    a_rows = flow_coords[:, :, 0]
    a_inner = flow_coords[:, :, 1]
    grp = g_inner // KA
    want = g_inner % KA
    rows_q = kept_row.T
    slot_a = jnp.argmax(
        a_rows[grp[:, None, :], :] == rows_q[:, :, None, None], axis=3
    ).astype(jnp.int32)
    have = a_inner[grp[:, None, :], slot_a] == want[:, None, :]
    moff = jnp.where(have, (grp[:, None, :] * rows_panel + slot_a) * tile, -1)

    flow_flat = flow_tiles.reshape(-1, tile)
    graph_flat = graph_tiles[g_tile.reshape(-1)].reshape(-1, tile)
    partial_sum = kept_partials(
        moff.reshape(-1).astype(jnp.int32),
        oidx.reshape(-1).astype(jnp.int32),
        flow_flat,
        graph_flat,
        n_out,
        layer_count,
        n_g,
    )
    kept_tiles = lax.psum_scatter(partial_sum, "layer", scatter_dimension=0, tiled=True)

    kept_cols = out_coords[0, 0, 0, :, 1]
    squared = kept_tiles * kept_tiles
    local_mass = jnp.sum(squared, axis=1)
    column_total = butterfly_sum(
        butterfly_sum(local_mass, "row", row_count, (1, 2)), "layer", layer_count, (1, 3)
    )
    factor = jnp.float32(row_count * layer_count * tile) / column_total
    flow = squared[kept_cols] * factor[kept_cols][:, None, :]
    return flow.reshape(1, 1, 1, col_tiles, tile, tile)


def solution(mesh):
    in_specs = (
        P("row", "col", "layer", None, None, None),
        P("row", "col", "layer", None, None),
        P("row", "col", "layer", None, None, None),
        P("row", "col", "layer", None, None),
        P("row", "col", "layer", None, None),
    )
    out_specs = P("row", "col", "layer", None, None, None)
    return jax.shard_map(local, mesh=mesh, in_specs=in_specs, out_specs=out_specs, check_vma=False)
```

```python
import functools

import jax
import jax.numpy as jnp
from jax import lax
from jax.experimental import pallas as pl
from jax.experimental.pallas import tpu as pltpu
from jax.sharding import PartitionSpec as P

KA = 4


def column_kernel(moff_ref, oidx_ref, flow_ref, graph_ref, out_ref, lhs_ref, *, n_q, n_g):
    tile = out_ref.shape[-1]
    n_col = out_ref.shape[0] // n_q

    lhs_ref[...] = jnp.zeros(lhs_ref.shape, lhs_ref.dtype)

    def each_block(j, action):
        for q in range(n_q):
            for g in range(n_g):
                m_off = moff_ref[(j * n_q + q) * n_g + g]

                @pl.when(m_off >= 0)
                def _():
                    action(q, g, m_off)

    def put(q, g, m_off):
        left = flow_ref[pl.ds(pl.multiple_of(m_off, tile), tile), :]
        lhs_ref[pl.ds(q * tile, tile), pl.ds(g * tile, tile)] = left

    def clear(q, g, m_off):
        lhs_ref[pl.ds(q * tile, tile), pl.ds(g * tile, tile)] = jnp.zeros((tile, tile), lhs_ref.dtype)

    def body(j, carry):
        each_block(j, put)
        right = graph_ref[pl.ds(pl.multiple_of(j * n_g * tile, n_g * tile), n_g * tile), :]
        res = jnp.dot(lhs_ref[...], right, preferred_element_type=jnp.float32)
        for q in range(n_q):
            out_ref[oidx_ref[j * n_q + q]] = res[q * tile : (q + 1) * tile]
        each_block(j, clear)
        return carry

    lax.fori_loop(0, n_col, body, 0)


def kept_partials(moff, oidx, flow_flat, graph_flat, n_out, n_q, n_g):
    tile = flow_flat.shape[-1]
    kernel = functools.partial(column_kernel, n_q=n_q, n_g=n_g)
    return pl.pallas_call(
        kernel,
        out_shape=jax.ShapeDtypeStruct((n_out, tile, tile), jnp.float32),
        in_specs=[
            pl.BlockSpec(memory_space=pltpu.SMEM),
            pl.BlockSpec(memory_space=pltpu.SMEM),
            pl.BlockSpec(memory_space=pltpu.VMEM),
            pl.BlockSpec(memory_space=pltpu.VMEM),
        ],
        out_specs=pl.BlockSpec(memory_space=pltpu.VMEM),
        scratch_shapes=[
            pltpu.VMEM((n_q * tile, n_g * tile), jnp.bfloat16),
        ],
        compiler_params=pltpu.CompilerParams(vmem_limit_bytes=48 * 1024 * 1024),
        cost_estimate=pl.CostEstimate(
            flops=2 * n_out * n_g * tile**3,
            transcendentals=0,
            bytes_accessed=2 * (flow_flat.size + graph_flat.size) + 4 * n_out * tile * tile,
        ),
    )(moff, oidx, flow_flat, graph_flat)


def butterfly_sum(x, axis, n, masks):
    for d in masks:
        x = x + lax.ppermute(x, axis, [(i, i ^ d) for i in range(n)])
    return x


def first_two(mask):
    n = mask.shape[-1]
    lo = jnp.argmax(mask, axis=-1).astype(jnp.int32)
    hi = (n - 1 - jnp.argmax(mask[..., ::-1], axis=-1)).astype(jnp.int32)
    return lo, hi


def local(a_tiles, a_coords, b_tiles, b_coords, out_coords):
    tile = a_tiles.shape[-1]
    rows_panel = a_tiles.shape[3]
    col_count = lax.axis_size("col")
    row_count = lax.axis_size("row")
    layer_count = lax.axis_size("layer")
    b_span = KA * col_count // row_count
    quarter = rows_panel // layer_count
    col_tiles = out_coords.shape[3]
    n_b = b_tiles.shape[3]
    my_row = lax.axis_index("row")

    own = b_tiles[0, 0, 0]
    far = lax.ppermute(own, "row", [(i, i ^ 2) for i in range(row_count)])
    near = lax.ppermute(own, "row", [(i, i ^ 1) for i in range(row_count)])
    far_near = lax.ppermute(far, "row", [(i, i ^ 1) for i in range(row_count)])
    graph_parts = [own, near, far, far_near]
    graph_tiles = jnp.concatenate(graph_parts, axis=0)
    graph_coords = lax.all_gather(b_coords[0, 0, 0][None], "row", axis=0, tiled=True)
    flow_tiles = lax.all_gather(a_tiles[0, 0, 0], "col", axis=0, tiled=True)
    flow_coords = lax.all_gather(a_coords[0, 0, 0][None], "col", axis=0, tiled=True)
    kept_all = lax.all_gather(out_coords[0, 0, 0][None], "layer", axis=0, tiled=True)

    n_out = layer_count * col_tiles
    col_ids = jnp.arange(col_tiles, dtype=jnp.int32)
    part_ids = jnp.arange(row_count, dtype=jnp.int32)
    owner_of_part = my_row ^ part_ids
    coords_by_part = graph_coords[owner_of_part]
    in_col = coords_by_part[:, None, :, 1] == col_ids[None, :, None]
    lo, hi = first_two(in_col)
    g_slot = jnp.stack([lo, hi], axis=2)
    g_b0 = jnp.take_along_axis(
        jnp.broadcast_to(coords_by_part[:, None, :, 0], in_col.shape), g_slot, axis=2
    )
    g_inner = owner_of_part[:, None, None] * b_span + g_b0
    g_tile = (part_ids[:, None, None] * n_b + g_slot).transpose(1, 0, 2).reshape(col_tiles, -1)
    g_inner = g_inner.transpose(1, 0, 2).reshape(col_tiles, -1)
    n_g = g_tile.shape[1]

    kept_here = kept_all[:, None, :, 1] == col_ids[None, :, None]
    kept_pos = jnp.argmax(kept_here, axis=2).astype(jnp.int32)
    kept_row0 = jnp.take_along_axis(kept_all[:, :, 0], kept_pos, axis=1)
    q_ids = jnp.arange(layer_count, dtype=jnp.int32)
    kept_row = q_ids[:, None] * quarter + kept_row0
    oidx = jnp.broadcast_to(q_ids[:, None] * col_tiles + col_ids[None, :], (layer_count, col_tiles)).T

    a_rows = flow_coords[:, :, 0]
    a_inner = flow_coords[:, :, 1]
    grp = g_inner // KA
    want = g_inner % KA
    rows_q = kept_row.T
    slot_a = jnp.argmax(
        a_rows[grp[:, None, :], :] == rows_q[:, :, None, None], axis=3
    ).astype(jnp.int32)
    have = a_inner[grp[:, None, :], slot_a] == want[:, None, :]
    moff = jnp.where(have, (grp[:, None, :] * rows_panel + slot_a) * tile, -1)

    flow_flat = flow_tiles.reshape(-1, tile)
    graph_flat = graph_tiles[g_tile.reshape(-1)].reshape(-1, tile)
    partial_sum = kept_partials(
        moff.reshape(-1).astype(jnp.int32),
        oidx.reshape(-1).astype(jnp.int32),
        flow_flat,
        graph_flat,
        n_out,
        layer_count,
        n_g,
    )
    kept_tiles = lax.psum_scatter(partial_sum, "layer", scatter_dimension=0, tiled=True)

    kept_cols = out_coords[0, 0, 0, :, 1]
    squared = kept_tiles * kept_tiles
    local_mass = jnp.sum(squared, axis=1)
    column_total = butterfly_sum(
        butterfly_sum(local_mass, "row", row_count, (1, 2)), "layer", layer_count, (1, 3)
    )
    factor = jnp.float32(row_count * layer_count * tile) / column_total
    flow = squared[kept_cols] * factor[kept_cols][:, None, :]
    return flow.reshape(1, 1, 1, col_tiles, tile, tile)


def solution(mesh):
    in_specs = (
        P("row", "col", "layer", None, None, None),
        P("row", "col", "layer", None, None),
        P("row", "col", "layer", None, None, None),
        P("row", "col", "layer", None, None),
        P("row", "col", "layer", None, None),
    )
    out_specs = P("row", "col", "layer", None, None, None)
    return jax.shard_map(local, mesh=mesh, in_specs=in_specs, out_specs=out_specs, check_vma=False)
```

```python
import functools

import jax
import jax.numpy as jnp
from jax import lax
from jax.experimental import pallas as pl
from jax.experimental.pallas import tpu as pltpu
from jax.sharding import PartitionSpec as P

KA = 4


def column_kernel(moff_ref, oidx_ref, flow_ref, graph_ref, out_ref, lhs_ref, *, n_q, n_g):
    tile = out_ref.shape[-1]
    n_col = out_ref.shape[0] // n_q

    def column(j, slot):
        for q in range(n_q):
            for g in range(n_g):
                m_off = moff_ref[(j * n_q + q) * n_g + g]
                left = flow_ref[pl.ds(pl.multiple_of(jnp.maximum(m_off, 0), tile), tile), :]
                left = jnp.where(m_off >= 0, left, jnp.zeros_like(left))
                lhs_ref[slot, pl.ds(q * tile, tile), pl.ds(g * tile, tile)] = left
        right = graph_ref[pl.ds(pl.multiple_of(j * n_g * tile, n_g * tile), n_g * tile), :]
        res = jnp.dot(lhs_ref[slot], right, preferred_element_type=jnp.float32)
        for q in range(n_q):
            out_ref[oidx_ref[j * n_q + q]] = res[q * tile : (q + 1) * tile]

    def body(i, carry):
        column(2 * i, 0)
        column(2 * i + 1, 1)
        return carry

    lax.fori_loop(0, n_col // 2, body, 0)


def kept_partials(moff, oidx, flow_flat, graph_flat, n_out, n_q, n_g):
    tile = flow_flat.shape[-1]
    kernel = functools.partial(column_kernel, n_q=n_q, n_g=n_g)
    return pl.pallas_call(
        kernel,
        out_shape=jax.ShapeDtypeStruct((n_out, tile, tile), jnp.float32),
        in_specs=[
            pl.BlockSpec(memory_space=pltpu.SMEM),
            pl.BlockSpec(memory_space=pltpu.SMEM),
            pl.BlockSpec(memory_space=pltpu.VMEM),
            pl.BlockSpec(memory_space=pltpu.VMEM),
        ],
        out_specs=pl.BlockSpec(memory_space=pltpu.VMEM),
        scratch_shapes=[
            pltpu.VMEM((2, n_q * tile, n_g * tile), jnp.bfloat16),
        ],
        compiler_params=pltpu.CompilerParams(vmem_limit_bytes=48 * 1024 * 1024),
        cost_estimate=pl.CostEstimate(
            flops=2 * n_out * n_g * tile**3,
            transcendentals=0,
            bytes_accessed=2 * (flow_flat.size + graph_flat.size) + 4 * n_out * tile * tile,
        ),
    )(moff, oidx, flow_flat, graph_flat)


def butterfly_sum(x, axis, n, masks):
    for d in masks:
        x = x + lax.ppermute(x, axis, [(i, i ^ d) for i in range(n)])
    return x


def first_two(mask):
    n = mask.shape[-1]
    lo = jnp.argmax(mask, axis=-1).astype(jnp.int32)
    hi = (n - 1 - jnp.argmax(mask[..., ::-1], axis=-1)).astype(jnp.int32)
    return lo, hi


def local(a_tiles, a_coords, b_tiles, b_coords, out_coords):
    tile = a_tiles.shape[-1]
    rows_panel = a_tiles.shape[3]
    col_count = lax.axis_size("col")
    row_count = lax.axis_size("row")
    layer_count = lax.axis_size("layer")
    b_span = KA * col_count // row_count
    quarter = rows_panel // layer_count
    col_tiles = out_coords.shape[3]
    n_b = b_tiles.shape[3]
    my_row = lax.axis_index("row")

    own = b_tiles[0, 0, 0]
    far = lax.ppermute(own, "row", [(i, i ^ 2) for i in range(row_count)])
    near = lax.ppermute(own, "row", [(i, i ^ 1) for i in range(row_count)])
    far_near = lax.ppermute(far, "row", [(i, i ^ 1) for i in range(row_count)])
    graph_parts = [own, near, far, far_near]
    graph_tiles = jnp.concatenate(graph_parts, axis=0)
    graph_coords = lax.all_gather(b_coords[0, 0, 0][None], "row", axis=0, tiled=True)
    flow_tiles = lax.all_gather(a_tiles[0, 0, 0], "col", axis=0, tiled=True)
    flow_coords = lax.all_gather(a_coords[0, 0, 0][None], "col", axis=0, tiled=True)
    kept_all = lax.all_gather(out_coords[0, 0, 0][None], "layer", axis=0, tiled=True)

    n_out = layer_count * col_tiles
    col_ids = jnp.arange(col_tiles, dtype=jnp.int32)
    part_ids = jnp.arange(row_count, dtype=jnp.int32)
    owner_of_part = my_row ^ part_ids
    coords_by_part = graph_coords[owner_of_part]
    in_col = coords_by_part[:, None, :, 1] == col_ids[None, :, None]
    lo, hi = first_two(in_col)
    g_slot = jnp.stack([lo, hi], axis=2)
    g_b0 = jnp.take_along_axis(
        jnp.broadcast_to(coords_by_part[:, None, :, 0], in_col.shape), g_slot, axis=2
    )
    g_inner = owner_of_part[:, None, None] * b_span + g_b0
    g_tile = (part_ids[:, None, None] * n_b + g_slot).transpose(1, 0, 2).reshape(col_tiles, -1)
    g_inner = g_inner.transpose(1, 0, 2).reshape(col_tiles, -1)
    n_g = g_tile.shape[1]

    kept_here = kept_all[:, None, :, 1] == col_ids[None, :, None]
    kept_pos = jnp.argmax(kept_here, axis=2).astype(jnp.int32)
    kept_row0 = jnp.take_along_axis(kept_all[:, :, 0], kept_pos, axis=1)
    q_ids = jnp.arange(layer_count, dtype=jnp.int32)
    kept_row = q_ids[:, None] * quarter + kept_row0
    oidx = jnp.broadcast_to(q_ids[:, None] * col_tiles + col_ids[None, :], (layer_count, col_tiles)).T

    a_rows = flow_coords[:, :, 0]
    a_inner = flow_coords[:, :, 1]
    grp = g_inner // KA
    want = g_inner % KA
    rows_q = kept_row.T
    slot_a = jnp.argmax(
        a_rows[grp[:, None, :], :] == rows_q[:, :, None, None], axis=3
    ).astype(jnp.int32)
    have = a_inner[grp[:, None, :], slot_a] == want[:, None, :]
    moff = jnp.where(have, (grp[:, None, :] * rows_panel + slot_a) * tile, -1)

    flow_flat = flow_tiles.reshape(-1, tile)
    graph_flat = graph_tiles[g_tile.reshape(-1)].reshape(-1, tile)
    partial_sum = kept_partials(
        moff.reshape(-1).astype(jnp.int32),
        oidx.reshape(-1).astype(jnp.int32),
        flow_flat,
        graph_flat,
        n_out,
        layer_count,
        n_g,
    )
    kept_tiles = lax.psum_scatter(partial_sum, "layer", scatter_dimension=0, tiled=True)

    kept_cols = out_coords[0, 0, 0, :, 1]
    squared = kept_tiles * kept_tiles
    local_mass = jnp.sum(squared, axis=1)
    column_total = butterfly_sum(
        butterfly_sum(local_mass, "row", row_count, (1, 2)), "layer", layer_count, (1, 3)
    )
    factor = jnp.float32(row_count * layer_count * tile) / column_total
    flow = squared[kept_cols] * factor[kept_cols][:, None, :]
    return flow.reshape(1, 1, 1, col_tiles, tile, tile)


def solution(mesh):
    in_specs = (
        P("row", "col", "layer", None, None, None),
        P("row", "col", "layer", None, None),
        P("row", "col", "layer", None, None, None),
        P("row", "col", "layer", None, None),
        P("row", "col", "layer", None, None),
    )
    out_specs = P("row", "col", "layer", None, None, None)
    return jax.shard_map(local, mesh=mesh, in_specs=in_specs, out_specs=out_specs, check_vma=False)
```

```python
import functools

import jax
import jax.numpy as jnp
from jax import lax
from jax.experimental import pallas as pl
from jax.experimental.pallas import tpu as pltpu
from jax.sharding import PartitionSpec as P

KA = 4
N_SLOT = 4


def column_kernel(moff_ref, oidx_ref, flow_ref, graph_ref, out_ref, lhs_ref, *, n_q, n_g):
    tile = out_ref.shape[-1]
    n_col = out_ref.shape[0] // n_q

    def column(j, slot):
        for q in range(n_q):
            for g in range(n_g):
                m_off = moff_ref[(j * n_q + q) * n_g + g]
                left = flow_ref[pl.ds(pl.multiple_of(jnp.maximum(m_off, 0), tile), tile), :]
                left = jnp.where(m_off >= 0, left, jnp.zeros_like(left))
                lhs_ref[slot, pl.ds(q * tile, tile), pl.ds(g * tile, tile)] = left
        right = graph_ref[pl.ds(pl.multiple_of(j * n_g * tile, n_g * tile), n_g * tile), :]
        res = jnp.dot(lhs_ref[slot], right, preferred_element_type=jnp.float32)
        for q in range(n_q):
            out_ref[oidx_ref[j * n_q + q]] = res[q * tile : (q + 1) * tile]

    def body(i, carry):
        for k in range(N_SLOT):
            column(N_SLOT * i + k, k)
        return carry

    lax.fori_loop(0, n_col // N_SLOT, body, 0)


def kept_partials(moff, oidx, flow_flat, graph_flat, n_out, n_q, n_g):
    tile = flow_flat.shape[-1]
    kernel = functools.partial(column_kernel, n_q=n_q, n_g=n_g)
    return pl.pallas_call(
        kernel,
        out_shape=jax.ShapeDtypeStruct((n_out, tile, tile), jnp.float32),
        in_specs=[
            pl.BlockSpec(memory_space=pltpu.SMEM),
            pl.BlockSpec(memory_space=pltpu.SMEM),
            pl.BlockSpec(memory_space=pltpu.VMEM),
            pl.BlockSpec(memory_space=pltpu.VMEM),
        ],
        out_specs=pl.BlockSpec(memory_space=pltpu.VMEM),
        scratch_shapes=[
            pltpu.VMEM((N_SLOT, n_q * tile, n_g * tile), jnp.bfloat16),
        ],
        compiler_params=pltpu.CompilerParams(vmem_limit_bytes=48 * 1024 * 1024),
        cost_estimate=pl.CostEstimate(
            flops=2 * n_out * n_g * tile**3,
            transcendentals=0,
            bytes_accessed=2 * (flow_flat.size + graph_flat.size) + 4 * n_out * tile * tile,
        ),
    )(moff, oidx, flow_flat, graph_flat)


def butterfly_sum(x, axis, n, masks):
    for d in masks:
        x = x + lax.ppermute(x, axis, [(i, i ^ d) for i in range(n)])
    return x


def first_two(mask):
    n = mask.shape[-1]
    lo = jnp.argmax(mask, axis=-1).astype(jnp.int32)
    hi = (n - 1 - jnp.argmax(mask[..., ::-1], axis=-1)).astype(jnp.int32)
    return lo, hi


def local(a_tiles, a_coords, b_tiles, b_coords, out_coords):
    tile = a_tiles.shape[-1]
    rows_panel = a_tiles.shape[3]
    col_count = lax.axis_size("col")
    row_count = lax.axis_size("row")
    layer_count = lax.axis_size("layer")
    b_span = KA * col_count // row_count
    quarter = rows_panel // layer_count
    col_tiles = out_coords.shape[3]
    n_b = b_tiles.shape[3]
    my_row = lax.axis_index("row")

    own = b_tiles[0, 0, 0]
    far = lax.ppermute(own, "row", [(i, i ^ 2) for i in range(row_count)])
    near = lax.ppermute(own, "row", [(i, i ^ 1) for i in range(row_count)])
    far_near = lax.ppermute(far, "row", [(i, i ^ 1) for i in range(row_count)])
    graph_parts = [own, near, far, far_near]
    graph_tiles = jnp.concatenate(graph_parts, axis=0)
    graph_coords = lax.all_gather(b_coords[0, 0, 0][None], "row", axis=0, tiled=True)
    flow_tiles = lax.all_gather(a_tiles[0, 0, 0], "col", axis=0, tiled=True)
    flow_coords = lax.all_gather(a_coords[0, 0, 0][None], "col", axis=0, tiled=True)
    kept_all = lax.all_gather(out_coords[0, 0, 0][None], "layer", axis=0, tiled=True)

    n_out = layer_count * col_tiles
    col_ids = jnp.arange(col_tiles, dtype=jnp.int32)
    part_ids = jnp.arange(row_count, dtype=jnp.int32)
    owner_of_part = my_row ^ part_ids
    coords_by_part = graph_coords[owner_of_part]
    in_col = coords_by_part[:, None, :, 1] == col_ids[None, :, None]
    lo, hi = first_two(in_col)
    g_slot = jnp.stack([lo, hi], axis=2)
    g_b0 = jnp.take_along_axis(
        jnp.broadcast_to(coords_by_part[:, None, :, 0], in_col.shape), g_slot, axis=2
    )
    g_inner = owner_of_part[:, None, None] * b_span + g_b0
    g_tile = (part_ids[:, None, None] * n_b + g_slot).transpose(1, 0, 2).reshape(col_tiles, -1)
    g_inner = g_inner.transpose(1, 0, 2).reshape(col_tiles, -1)
    n_g = g_tile.shape[1]

    kept_here = kept_all[:, None, :, 1] == col_ids[None, :, None]
    kept_pos = jnp.argmax(kept_here, axis=2).astype(jnp.int32)
    kept_row0 = jnp.take_along_axis(kept_all[:, :, 0], kept_pos, axis=1)
    q_ids = jnp.arange(layer_count, dtype=jnp.int32)
    kept_row = q_ids[:, None] * quarter + kept_row0
    oidx = jnp.broadcast_to(q_ids[:, None] * col_tiles + col_ids[None, :], (layer_count, col_tiles)).T

    a_rows = flow_coords[:, :, 0]
    a_inner = flow_coords[:, :, 1]
    grp = g_inner // KA
    want = g_inner % KA
    rows_q = kept_row.T
    slot_a = jnp.argmax(
        a_rows[grp[:, None, :], :] == rows_q[:, :, None, None], axis=3
    ).astype(jnp.int32)
    have = a_inner[grp[:, None, :], slot_a] == want[:, None, :]
    moff = jnp.where(have, (grp[:, None, :] * rows_panel + slot_a) * tile, -1)

    flow_flat = flow_tiles.reshape(-1, tile)
    graph_flat = graph_tiles[g_tile.reshape(-1)].reshape(-1, tile)
    partial_sum = kept_partials(
        moff.reshape(-1).astype(jnp.int32),
        oidx.reshape(-1).astype(jnp.int32),
        flow_flat,
        graph_flat,
        n_out,
        layer_count,
        n_g,
    )
    kept_tiles = lax.psum_scatter(partial_sum, "layer", scatter_dimension=0, tiled=True)

    kept_cols = out_coords[0, 0, 0, :, 1]
    squared = kept_tiles * kept_tiles
    local_mass = jnp.sum(squared, axis=1)
    column_total = butterfly_sum(
        butterfly_sum(local_mass, "row", row_count, (1, 2)), "layer", layer_count, (1, 3)
    )
    factor = jnp.float32(row_count * layer_count * tile) / column_total
    flow = squared[kept_cols] * factor[kept_cols][:, None, :]
    return flow.reshape(1, 1, 1, col_tiles, tile, tile)


def solution(mesh):
    in_specs = (
        P("row", "col", "layer", None, None, None),
        P("row", "col", "layer", None, None),
        P("row", "col", "layer", None, None, None),
        P("row", "col", "layer", None, None),
        P("row", "col", "layer", None, None),
    )
    out_specs = P("row", "col", "layer", None, None, None)
    return jax.shard_map(local, mesh=mesh, in_specs=in_specs, out_specs=out_specs, check_vma=False)
```

```python
import functools

import jax
import jax.numpy as jnp
from jax import lax
from jax.experimental import pallas as pl
from jax.experimental.pallas import tpu as pltpu
from jax.sharding import PartitionSpec as P

KA = 4
N_SLOT = 4


def column_kernel(moff_ref, oidx_ref, flow_ref, graph_hbm, out_ref, lhs_ref, graph_ref, graph_sem, *, n_q, n_g):
    tile = out_ref.shape[-1]
    n_col = out_ref.shape[0] // n_q

    def column(j, slot):
        for q in range(n_q):
            for g in range(n_g):
                m_off = moff_ref[(j * n_q + q) * n_g + g]
                left = flow_ref[pl.ds(pl.multiple_of(jnp.maximum(m_off, 0), tile), tile), :]
                left = jnp.where(m_off >= 0, left, jnp.zeros_like(left))
                lhs_ref[slot, pl.ds(q * tile, tile), pl.ds(g * tile, tile)] = left
        right = graph_ref[pl.ds(pl.multiple_of(j * n_g * tile, n_g * tile), n_g * tile), :]
        res = jnp.dot(lhs_ref[slot], right, preferred_element_type=jnp.float32)
        for q in range(n_q):
            out_ref[oidx_ref[j * n_q + q]] = res[q * tile : (q + 1) * tile]

    chunk = N_SLOT * n_g * tile
    n_step = n_col // N_SLOT
    copies = [
        pltpu.make_async_copy(
            graph_hbm.at[pl.ds(i * chunk, chunk), :], graph_ref.at[pl.ds(i * chunk, chunk), :], graph_sem.at[i]
        )
        for i in range(n_step)
    ]
    for copy in copies:
        copy.start()

    def body(i, carry):
        for k in range(N_SLOT):
            column(N_SLOT * i + k, k)
        return carry

    for i in range(n_step):
        copies[i].wait()
        body(i, 0)


def kept_partials(moff, oidx, flow_flat, graph_flat, n_out, n_q, n_g):
    tile = flow_flat.shape[-1]
    kernel = functools.partial(column_kernel, n_q=n_q, n_g=n_g)
    return pl.pallas_call(
        kernel,
        out_shape=jax.ShapeDtypeStruct((n_out, tile, tile), jnp.float32),
        in_specs=[
            pl.BlockSpec(memory_space=pltpu.SMEM),
            pl.BlockSpec(memory_space=pltpu.SMEM),
            pl.BlockSpec(memory_space=pltpu.VMEM),
            pl.BlockSpec(memory_space=pl.ANY),
        ],
        out_specs=pl.BlockSpec(memory_space=pltpu.VMEM),
        scratch_shapes=[
            pltpu.VMEM((N_SLOT, n_q * tile, n_g * tile), jnp.bfloat16),
            pltpu.VMEM(graph_flat.shape, jnp.bfloat16),
            pltpu.SemaphoreType.DMA((n_out // n_q // N_SLOT,)),
        ],
        compiler_params=pltpu.CompilerParams(vmem_limit_bytes=48 * 1024 * 1024),
        cost_estimate=pl.CostEstimate(
            flops=2 * n_out * n_g * tile**3,
            transcendentals=0,
            bytes_accessed=2 * (flow_flat.size + graph_flat.size) + 4 * n_out * tile * tile,
        ),
    )(moff, oidx, flow_flat, graph_flat)


def butterfly_sum(x, axis, n, masks):
    for d in masks:
        x = x + lax.ppermute(x, axis, [(i, i ^ d) for i in range(n)])
    return x


def first_two(mask):
    n = mask.shape[-1]
    lo = jnp.argmax(mask, axis=-1).astype(jnp.int32)
    hi = (n - 1 - jnp.argmax(mask[..., ::-1], axis=-1)).astype(jnp.int32)
    return lo, hi


def local(a_tiles, a_coords, b_tiles, b_coords, out_coords):
    tile = a_tiles.shape[-1]
    rows_panel = a_tiles.shape[3]
    col_count = lax.axis_size("col")
    row_count = lax.axis_size("row")
    layer_count = lax.axis_size("layer")
    b_span = KA * col_count // row_count
    quarter = rows_panel // layer_count
    col_tiles = out_coords.shape[3]
    n_b = b_tiles.shape[3]
    my_row = lax.axis_index("row")

    own = b_tiles[0, 0, 0]
    far = lax.ppermute(own, "row", [(i, i ^ 2) for i in range(row_count)])
    near = lax.ppermute(own, "row", [(i, i ^ 1) for i in range(row_count)])
    far_near = lax.ppermute(far, "row", [(i, i ^ 1) for i in range(row_count)])
    graph_parts = [own, near, far, far_near]
    graph_tiles = jnp.concatenate(graph_parts, axis=0)
    graph_coords = lax.all_gather(b_coords[0, 0, 0][None], "row", axis=0, tiled=True)
    flow_tiles = lax.all_gather(a_tiles[0, 0, 0], "col", axis=0, tiled=True)
    flow_coords = lax.all_gather(a_coords[0, 0, 0][None], "col", axis=0, tiled=True)
    kept_all = lax.all_gather(out_coords[0, 0, 0][None], "layer", axis=0, tiled=True)

    n_out = layer_count * col_tiles
    col_ids = jnp.arange(col_tiles, dtype=jnp.int32)
    part_ids = jnp.arange(row_count, dtype=jnp.int32)
    owner_of_part = my_row ^ part_ids
    coords_by_part = graph_coords[owner_of_part]
    in_col = coords_by_part[:, None, :, 1] == col_ids[None, :, None]
    lo, hi = first_two(in_col)
    g_slot = jnp.stack([lo, hi], axis=2)
    g_b0 = jnp.take_along_axis(
        jnp.broadcast_to(coords_by_part[:, None, :, 0], in_col.shape), g_slot, axis=2
    )
    g_inner = owner_of_part[:, None, None] * b_span + g_b0
    g_tile = (part_ids[:, None, None] * n_b + g_slot).transpose(1, 0, 2).reshape(col_tiles, -1)
    g_inner = g_inner.transpose(1, 0, 2).reshape(col_tiles, -1)
    n_g = g_tile.shape[1]

    kept_here = kept_all[:, None, :, 1] == col_ids[None, :, None]
    kept_pos = jnp.argmax(kept_here, axis=2).astype(jnp.int32)
    kept_row0 = jnp.take_along_axis(kept_all[:, :, 0], kept_pos, axis=1)
    q_ids = jnp.arange(layer_count, dtype=jnp.int32)
    kept_row = q_ids[:, None] * quarter + kept_row0
    oidx = jnp.broadcast_to(q_ids[:, None] * col_tiles + col_ids[None, :], (layer_count, col_tiles)).T

    a_rows = flow_coords[:, :, 0]
    a_inner = flow_coords[:, :, 1]
    grp = g_inner // KA
    want = g_inner % KA
    rows_q = kept_row.T
    slot_a = jnp.argmax(
        a_rows[grp[:, None, :], :] == rows_q[:, :, None, None], axis=3
    ).astype(jnp.int32)
    have = a_inner[grp[:, None, :], slot_a] == want[:, None, :]
    moff = jnp.where(have, (grp[:, None, :] * rows_panel + slot_a) * tile, -1)

    flow_flat = flow_tiles.reshape(-1, tile)
    graph_flat = graph_tiles[g_tile.reshape(-1)].reshape(-1, tile)
    partial_sum = kept_partials(
        moff.reshape(-1).astype(jnp.int32),
        oidx.reshape(-1).astype(jnp.int32),
        flow_flat,
        graph_flat,
        n_out,
        layer_count,
        n_g,
    )
    kept_tiles = lax.psum_scatter(partial_sum, "layer", scatter_dimension=0, tiled=True)

    kept_cols = out_coords[0, 0, 0, :, 1]
    squared = kept_tiles * kept_tiles
    local_mass = jnp.sum(squared, axis=1)
    column_total = butterfly_sum(
        butterfly_sum(local_mass, "row", row_count, (1, 2)), "layer", layer_count, (1, 3)
    )
    factor = jnp.float32(row_count * layer_count * tile) / column_total
    flow = squared[kept_cols] * factor[kept_cols][:, None, :]
    return flow.reshape(1, 1, 1, col_tiles, tile, tile)


def solution(mesh):
    in_specs = (
        P("row", "col", "layer", None, None, None),
        P("row", "col", "layer", None, None),
        P("row", "col", "layer", None, None, None),
        P("row", "col", "layer", None, None),
        P("row", "col", "layer", None, None),
    )
    out_specs = P("row", "col", "layer", None, None, None)
    return jax.shard_map(local, mesh=mesh, in_specs=in_specs, out_specs=out_specs, check_vma=False)
```

```python
import functools

import jax
import jax.numpy as jnp
from jax import lax
from jax.experimental import pallas as pl
from jax.experimental.pallas import tpu as pltpu
from jax.sharding import PartitionSpec as P

KA = 4
N_SLOT = 4


def column_kernel(moff_ref, oidx_ref, flow_ref, graph_ref, out_ref, lhs_ref, *, n_q, n_g):
    tile = out_ref.shape[-1]
    n_col = out_ref.shape[0] // n_q

    def column(j, slot):
        for q in range(n_q):
            for g in range(n_g):
                m_off = moff_ref[(j * n_q + q) * n_g + g]
                left = flow_ref[pl.ds(pl.multiple_of(jnp.maximum(m_off, 0), tile), tile), :]
                left = jnp.where(m_off >= 0, left, jnp.zeros_like(left))
                lhs_ref[slot, pl.ds(q * tile, tile), pl.ds(g * tile, tile)] = left
        right = graph_ref[pl.ds(pl.multiple_of(j * n_g * tile, n_g * tile), n_g * tile), :]
        res = jnp.dot(lhs_ref[slot], right, preferred_element_type=jnp.float32)
        for q in range(n_q):
            out_ref[oidx_ref[j * n_q + q]] = res[q * tile : (q + 1) * tile]

    def body(i, carry):
        for k in range(N_SLOT):
            column(N_SLOT * i + k, k)
        return carry

    lax.fori_loop(0, n_col // N_SLOT, body, 0)


def kept_partials(moff, oidx, flow_flat, graph_flat, n_out, n_q, n_g):
    tile = flow_flat.shape[-1]
    kernel = functools.partial(column_kernel, n_q=n_q, n_g=n_g)
    return pl.pallas_call(
        kernel,
        out_shape=jax.ShapeDtypeStruct((n_out, tile, tile), jnp.float32),
        in_specs=[
            pl.BlockSpec(memory_space=pltpu.SMEM),
            pl.BlockSpec(memory_space=pltpu.SMEM),
            pl.BlockSpec(memory_space=pltpu.VMEM),
            pl.BlockSpec(memory_space=pltpu.VMEM),
        ],
        out_specs=pl.BlockSpec(memory_space=pltpu.VMEM),
        scratch_shapes=[
            pltpu.VMEM((N_SLOT, n_q * tile, n_g * tile), jnp.bfloat16),
        ],
        compiler_params=pltpu.CompilerParams(vmem_limit_bytes=48 * 1024 * 1024),
        cost_estimate=pl.CostEstimate(
            flops=2 * n_out * n_g * tile**3,
            transcendentals=0,
            bytes_accessed=2 * (flow_flat.size + graph_flat.size) + 4 * n_out * tile * tile,
        ),
    )(moff, oidx, flow_flat, graph_flat)


def butterfly_sum(x, axis, n, masks):
    for d in masks:
        x = x + lax.ppermute(x, axis, [(i, i ^ d) for i in range(n)])
    return x


def first_two(mask):
    n = mask.shape[-1]
    lo = jnp.argmax(mask, axis=-1).astype(jnp.int32)
    hi = (n - 1 - jnp.argmax(mask[..., ::-1], axis=-1)).astype(jnp.int32)
    return lo, hi


def local(a_tiles, a_coords, b_tiles, b_coords, out_coords):
    tile = a_tiles.shape[-1]
    rows_panel = a_tiles.shape[3]
    col_count = lax.axis_size("col")
    row_count = lax.axis_size("row")
    layer_count = lax.axis_size("layer")
    b_span = KA * col_count // row_count
    quarter = rows_panel // layer_count
    col_tiles = out_coords.shape[3]
    n_b = b_tiles.shape[3]
    my_row = lax.axis_index("row")

    own = b_tiles[0, 0, 0]
    far = lax.ppermute(own, "row", [(i, i ^ 2) for i in range(row_count)])
    near = lax.ppermute(own, "row", [(i, i ^ 1) for i in range(row_count)])
    far_near = lax.ppermute(far, "row", [(i, i ^ 1) for i in range(row_count)])
    graph_parts = [own, near, far, far_near]
    graph_tiles = jnp.concatenate(graph_parts, axis=0)
    graph_coords = lax.all_gather(b_coords[0, 0, 0][None], "row", axis=0, tiled=True)
    flow_tiles = lax.all_gather(a_tiles[0, 0, 0], "col", axis=0, tiled=True)
    flow_coords = lax.all_gather(a_coords[0, 0, 0][None], "col", axis=0, tiled=True)
    kept_all = lax.all_gather(out_coords[0, 0, 0][None], "layer", axis=0, tiled=True)

    n_out = layer_count * col_tiles
    col_ids = jnp.arange(col_tiles, dtype=jnp.int32)
    part_ids = jnp.arange(row_count, dtype=jnp.int32)
    owner_of_part = my_row ^ part_ids
    coords_by_part = graph_coords[owner_of_part]
    in_col = coords_by_part[:, None, :, 1] == col_ids[None, :, None]
    lo, hi = first_two(in_col)
    g_slot = jnp.stack([lo, hi], axis=2)
    g_b0 = jnp.take_along_axis(
        jnp.broadcast_to(coords_by_part[:, None, :, 0], in_col.shape), g_slot, axis=2
    )
    g_inner = owner_of_part[:, None, None] * b_span + g_b0
    g_tile = (part_ids[:, None, None] * n_b + g_slot).transpose(1, 0, 2).reshape(col_tiles, -1)
    g_inner = g_inner.transpose(1, 0, 2).reshape(col_tiles, -1)
    n_g = g_tile.shape[1]

    kept_here = kept_all[:, None, :, 1] == col_ids[None, :, None]
    kept_pos = jnp.argmax(kept_here, axis=2).astype(jnp.int32)
    kept_row0 = jnp.take_along_axis(kept_all[:, :, 0], kept_pos, axis=1)
    q_ids = jnp.arange(layer_count, dtype=jnp.int32)
    kept_row = q_ids[:, None] * quarter + kept_row0
    oidx = jnp.broadcast_to(q_ids[:, None] * col_tiles + col_ids[None, :], (layer_count, col_tiles)).T

    a_rows = flow_coords[:, :, 0]
    a_inner = flow_coords[:, :, 1]
    grp = g_inner // KA
    want = g_inner % KA
    rows_q = kept_row.T
    slot_a = jnp.argmax(
        a_rows[grp[:, None, :], :] == rows_q[:, :, None, None], axis=3
    ).astype(jnp.int32)
    have = a_inner[grp[:, None, :], slot_a] == want[:, None, :]
    moff = jnp.where(have, (grp[:, None, :] * rows_panel + slot_a) * tile, -1)

    flow_flat = flow_tiles.reshape(-1, tile)
    graph_flat = graph_tiles[g_tile.reshape(-1)].reshape(-1, tile)
    partial_sum = kept_partials(
        moff.reshape(-1).astype(jnp.int32),
        oidx.reshape(-1).astype(jnp.int32),
        flow_flat,
        graph_flat,
        n_out,
        layer_count,
        n_g,
    )
    kept_tiles = lax.psum_scatter(partial_sum, "layer", scatter_dimension=0, tiled=True)

    kept_cols = out_coords[0, 0, 0, :, 1]
    squared = kept_tiles * kept_tiles
    local_mass = jnp.sum(squared, axis=1)
    row_parts = [lax.ppermute(local_mass, "row", [(i, i ^ d) for i in range(row_count)]) for d in range(1, row_count)]
    row_total = local_mass + sum(row_parts[1:], row_parts[0])
    column_total = butterfly_sum(row_total, "layer", layer_count, (1, 3))
    factor = jnp.float32(row_count * layer_count * tile) / column_total
    flow = squared[kept_cols] * factor[kept_cols][:, None, :]
    return flow.reshape(1, 1, 1, col_tiles, tile, tile)


def solution(mesh):
    in_specs = (
        P("row", "col", "layer", None, None, None),
        P("row", "col", "layer", None, None),
        P("row", "col", "layer", None, None, None),
        P("row", "col", "layer", None, None),
        P("row", "col", "layer", None, None),
    )
    out_specs = P("row", "col", "layer", None, None, None)
    return jax.shard_map(local, mesh=mesh, in_specs=in_specs, out_specs=out_specs, check_vma=False)
```

```python
import functools

import jax
import jax.numpy as jnp
from jax import lax
from jax.experimental import pallas as pl
from jax.experimental.pallas import tpu as pltpu
from jax.sharding import PartitionSpec as P

KA = 4
N_SLOT = 4


def column_kernel(moff_ref, oidx_ref, flow_ref, graph_ref, out_ref, lhs_ref, *, n_q, n_g):
    tile = out_ref.shape[-1]
    n_col = out_ref.shape[0] // n_q

    def column(j, slot):
        for q in range(n_q):
            for g in range(n_g):
                m_off = moff_ref[(j * n_q + q) * n_g + g]
                left = flow_ref[pl.ds(pl.multiple_of(jnp.maximum(m_off, 0), tile), tile), :]
                left = jnp.where(m_off >= 0, left, jnp.zeros_like(left))
                lhs_ref[slot, pl.ds(q * tile, tile), pl.ds(g * tile, tile)] = left
        right = graph_ref[pl.ds(pl.multiple_of(j * n_g * tile, n_g * tile), n_g * tile), :]
        res = jnp.dot(lhs_ref[slot], right, preferred_element_type=jnp.float32)
        for q in range(n_q):
            out_ref[oidx_ref[j * n_q + q]] = res[q * tile : (q + 1) * tile]

    def body(i, carry):
        for k in range(N_SLOT):
            column(N_SLOT * i + k, k)
        return carry

    lax.fori_loop(0, n_col // N_SLOT, body, 0)


def kept_partials(moff, oidx, flow_flat, graph_flat, n_out, n_q, n_g):
    tile = flow_flat.shape[-1]
    kernel = functools.partial(column_kernel, n_q=n_q, n_g=n_g)
    return pl.pallas_call(
        kernel,
        out_shape=jax.ShapeDtypeStruct((n_out, tile, tile), jnp.float32),
        in_specs=[
            pl.BlockSpec(memory_space=pltpu.SMEM),
            pl.BlockSpec(memory_space=pltpu.SMEM),
            pl.BlockSpec(memory_space=pltpu.VMEM),
            pl.BlockSpec(memory_space=pltpu.VMEM),
        ],
        out_specs=pl.BlockSpec(memory_space=pltpu.VMEM),
        scratch_shapes=[
            pltpu.VMEM((N_SLOT, n_q * tile, n_g * tile), jnp.bfloat16),
        ],
        compiler_params=pltpu.CompilerParams(vmem_limit_bytes=48 * 1024 * 1024),
        cost_estimate=pl.CostEstimate(
            flops=2 * n_out * n_g * tile**3,
            transcendentals=0,
            bytes_accessed=2 * (flow_flat.size + graph_flat.size) + 4 * n_out * tile * tile,
        ),
    )(moff, oidx, flow_flat, graph_flat)


def round_sum(x, axis, n):
    parts = [lax.ppermute(x, axis, [(i, i ^ d) for i in range(n)]) for d in range(1, n)]
    return x + sum(parts[1:], parts[0])


def first_two(mask):
    n = mask.shape[-1]
    lo = jnp.argmax(mask, axis=-1).astype(jnp.int32)
    hi = (n - 1 - jnp.argmax(mask[..., ::-1], axis=-1)).astype(jnp.int32)
    return lo, hi


def local(a_tiles, a_coords, b_tiles, b_coords, out_coords):
    tile = a_tiles.shape[-1]
    rows_panel = a_tiles.shape[3]
    col_count = lax.axis_size("col")
    row_count = lax.axis_size("row")
    layer_count = lax.axis_size("layer")
    b_span = KA * col_count // row_count
    quarter = rows_panel // layer_count
    col_tiles = out_coords.shape[3]
    n_b = b_tiles.shape[3]
    my_row = lax.axis_index("row")

    own = b_tiles[0, 0, 0]
    far = lax.ppermute(own, "row", [(i, i ^ 2) for i in range(row_count)])
    near = lax.ppermute(own, "row", [(i, i ^ 1) for i in range(row_count)])
    far_near = lax.ppermute(far, "row", [(i, i ^ 1) for i in range(row_count)])
    graph_parts = [own, near, far, far_near]
    graph_tiles = jnp.concatenate(graph_parts, axis=0)
    graph_coords = lax.all_gather(b_coords[0, 0, 0][None], "row", axis=0, tiled=True)
    flow_tiles = lax.all_gather(a_tiles[0, 0, 0], "col", axis=0, tiled=True)
    flow_coords = lax.all_gather(a_coords[0, 0, 0][None], "col", axis=0, tiled=True)
    kept_all = lax.all_gather(out_coords[0, 0, 0][None], "layer", axis=0, tiled=True)

    n_out = layer_count * col_tiles
    col_ids = jnp.arange(col_tiles, dtype=jnp.int32)
    part_ids = jnp.arange(row_count, dtype=jnp.int32)
    owner_of_part = my_row ^ part_ids
    coords_by_part = graph_coords[owner_of_part]
    in_col = coords_by_part[:, None, :, 1] == col_ids[None, :, None]
    lo, hi = first_two(in_col)
    g_slot = jnp.stack([lo, hi], axis=2)
    g_b0 = jnp.take_along_axis(
        jnp.broadcast_to(coords_by_part[:, None, :, 0], in_col.shape), g_slot, axis=2
    )
    g_inner = owner_of_part[:, None, None] * b_span + g_b0
    g_tile = (part_ids[:, None, None] * n_b + g_slot).transpose(1, 0, 2).reshape(col_tiles, -1)
    g_inner = g_inner.transpose(1, 0, 2).reshape(col_tiles, -1)
    n_g = g_tile.shape[1]

    kept_here = kept_all[:, None, :, 1] == col_ids[None, :, None]
    kept_pos = jnp.argmax(kept_here, axis=2).astype(jnp.int32)
    kept_row0 = jnp.take_along_axis(kept_all[:, :, 0], kept_pos, axis=1)
    q_ids = jnp.arange(layer_count, dtype=jnp.int32)
    kept_row = q_ids[:, None] * quarter + kept_row0
    oidx = jnp.broadcast_to(q_ids[:, None] * col_tiles + col_ids[None, :], (layer_count, col_tiles)).T

    a_rows = flow_coords[:, :, 0]
    a_inner = flow_coords[:, :, 1]
    grp = g_inner // KA
    want = g_inner % KA
    rows_q = kept_row.T
    slot_a = jnp.argmax(
        a_rows[grp[:, None, :], :] == rows_q[:, :, None, None], axis=3
    ).astype(jnp.int32)
    have = a_inner[grp[:, None, :], slot_a] == want[:, None, :]
    moff = jnp.where(have, (grp[:, None, :] * rows_panel + slot_a) * tile, -1)

    flow_flat = flow_tiles.reshape(-1, tile)
    graph_flat = graph_tiles[g_tile.reshape(-1)].reshape(-1, tile)
    partial_sum = kept_partials(
        moff.reshape(-1).astype(jnp.int32),
        oidx.reshape(-1).astype(jnp.int32),
        flow_flat,
        graph_flat,
        n_out,
        layer_count,
        n_g,
    )
    kept_tiles = lax.psum_scatter(partial_sum, "layer", scatter_dimension=0, tiled=True)

    kept_cols = out_coords[0, 0, 0, :, 1]
    squared = kept_tiles * kept_tiles
    local_mass = jnp.sum(squared, axis=1)
    column_total = round_sum(round_sum(local_mass, "row", row_count), "layer", layer_count)
    factor = jnp.float32(row_count * layer_count * tile) / column_total
    flow = squared[kept_cols] * factor[kept_cols][:, None, :]
    return flow.reshape(1, 1, 1, col_tiles, tile, tile)


def solution(mesh):
    in_specs = (
        P("row", "col", "layer", None, None, None),
        P("row", "col", "layer", None, None),
        P("row", "col", "layer", None, None, None),
        P("row", "col", "layer", None, None),
        P("row", "col", "layer", None, None),
    )
    out_specs = P("row", "col", "layer", None, None, None)
    return jax.shard_map(local, mesh=mesh, in_specs=in_specs, out_specs=out_specs, check_vma=False)
```

```python
import functools

import jax
import jax.numpy as jnp
from jax import lax
from jax.experimental import pallas as pl
from jax.experimental.pallas import tpu as pltpu
from jax.sharding import PartitionSpec as P

KA = 4
N_SLOT = 8


def column_kernel(moff_ref, oidx_ref, flow_ref, graph_ref, out_ref, lhs_ref, *, n_q, n_g):
    tile = out_ref.shape[-1]
    n_col = out_ref.shape[0] // n_q

    def column(j, slot):
        for q in range(n_q):
            for g in range(n_g):
                m_off = moff_ref[(j * n_q + q) * n_g + g]
                left = flow_ref[pl.ds(pl.multiple_of(jnp.maximum(m_off, 0), tile), tile), :]
                left = jnp.where(m_off >= 0, left, jnp.zeros_like(left))
                lhs_ref[slot, pl.ds(q * tile, tile), pl.ds(g * tile, tile)] = left
        right = graph_ref[pl.ds(pl.multiple_of(j * n_g * tile, n_g * tile), n_g * tile), :]
        res = jnp.dot(lhs_ref[slot], right, preferred_element_type=jnp.float32)
        for q in range(n_q):
            out_ref[oidx_ref[j * n_q + q]] = res[q * tile : (q + 1) * tile]

    def body(i, carry):
        for k in range(N_SLOT):
            column(N_SLOT * i + k, k)
        return carry

    lax.fori_loop(0, n_col // N_SLOT, body, 0)


def kept_partials(moff, oidx, flow_flat, graph_flat, n_out, n_q, n_g):
    tile = flow_flat.shape[-1]
    kernel = functools.partial(column_kernel, n_q=n_q, n_g=n_g)
    return pl.pallas_call(
        kernel,
        out_shape=jax.ShapeDtypeStruct((n_out, tile, tile), jnp.float32),
        in_specs=[
            pl.BlockSpec(memory_space=pltpu.SMEM),
            pl.BlockSpec(memory_space=pltpu.SMEM),
            pl.BlockSpec(memory_space=pltpu.VMEM),
            pl.BlockSpec(memory_space=pltpu.VMEM),
        ],
        out_specs=pl.BlockSpec(memory_space=pltpu.VMEM),
        scratch_shapes=[
            pltpu.VMEM((N_SLOT, n_q * tile, n_g * tile), jnp.bfloat16),
        ],
        compiler_params=pltpu.CompilerParams(vmem_limit_bytes=48 * 1024 * 1024),
        cost_estimate=pl.CostEstimate(
            flops=2 * n_out * n_g * tile**3,
            transcendentals=0,
            bytes_accessed=2 * (flow_flat.size + graph_flat.size) + 4 * n_out * tile * tile,
        ),
    )(moff, oidx, flow_flat, graph_flat)


def round_sum(x, axis, n):
    parts = [lax.ppermute(x, axis, [(i, i ^ d) for i in range(n)]) for d in range(1, n)]
    return x + sum(parts[1:], parts[0])


def first_two(mask):
    n = mask.shape[-1]
    lo = jnp.argmax(mask, axis=-1).astype(jnp.int32)
    hi = (n - 1 - jnp.argmax(mask[..., ::-1], axis=-1)).astype(jnp.int32)
    return lo, hi


def local(a_tiles, a_coords, b_tiles, b_coords, out_coords):
    tile = a_tiles.shape[-1]
    rows_panel = a_tiles.shape[3]
    col_count = lax.axis_size("col")
    row_count = lax.axis_size("row")
    layer_count = lax.axis_size("layer")
    b_span = KA * col_count // row_count
    quarter = rows_panel // layer_count
    col_tiles = out_coords.shape[3]
    n_b = b_tiles.shape[3]
    my_row = lax.axis_index("row")

    own = b_tiles[0, 0, 0]
    far = lax.ppermute(own, "row", [(i, i ^ 2) for i in range(row_count)])
    near = lax.ppermute(own, "row", [(i, i ^ 1) for i in range(row_count)])
    far_near = lax.ppermute(far, "row", [(i, i ^ 1) for i in range(row_count)])
    graph_parts = [own, near, far, far_near]
    graph_tiles = jnp.concatenate(graph_parts, axis=0)
    graph_coords = lax.all_gather(b_coords[0, 0, 0][None], "row", axis=0, tiled=True)
    flow_tiles = lax.all_gather(a_tiles[0, 0, 0], "col", axis=0, tiled=True)
    flow_coords = lax.all_gather(a_coords[0, 0, 0][None], "col", axis=0, tiled=True)
    kept_all = lax.all_gather(out_coords[0, 0, 0][None], "layer", axis=0, tiled=True)

    n_out = layer_count * col_tiles
    col_ids = jnp.arange(col_tiles, dtype=jnp.int32)
    part_ids = jnp.arange(row_count, dtype=jnp.int32)
    owner_of_part = my_row ^ part_ids
    coords_by_part = graph_coords[owner_of_part]
    in_col = coords_by_part[:, None, :, 1] == col_ids[None, :, None]
    lo, hi = first_two(in_col)
    g_slot = jnp.stack([lo, hi], axis=2)
    g_b0 = jnp.take_along_axis(
        jnp.broadcast_to(coords_by_part[:, None, :, 0], in_col.shape), g_slot, axis=2
    )
    g_inner = owner_of_part[:, None, None] * b_span + g_b0
    g_tile = (part_ids[:, None, None] * n_b + g_slot).transpose(1, 0, 2).reshape(col_tiles, -1)
    g_inner = g_inner.transpose(1, 0, 2).reshape(col_tiles, -1)
    n_g = g_tile.shape[1]

    kept_here = kept_all[:, None, :, 1] == col_ids[None, :, None]
    kept_pos = jnp.argmax(kept_here, axis=2).astype(jnp.int32)
    kept_row0 = jnp.take_along_axis(kept_all[:, :, 0], kept_pos, axis=1)
    q_ids = jnp.arange(layer_count, dtype=jnp.int32)
    kept_row = q_ids[:, None] * quarter + kept_row0
    oidx = jnp.broadcast_to(q_ids[:, None] * col_tiles + col_ids[None, :], (layer_count, col_tiles)).T

    a_rows = flow_coords[:, :, 0]
    a_inner = flow_coords[:, :, 1]
    grp = g_inner // KA
    want = g_inner % KA
    rows_q = kept_row.T
    slot_a = jnp.argmax(
        a_rows[grp[:, None, :], :] == rows_q[:, :, None, None], axis=3
    ).astype(jnp.int32)
    have = a_inner[grp[:, None, :], slot_a] == want[:, None, :]
    moff = jnp.where(have, (grp[:, None, :] * rows_panel + slot_a) * tile, -1)

    flow_flat = flow_tiles.reshape(-1, tile)
    graph_flat = graph_tiles[g_tile.reshape(-1)].reshape(-1, tile)
    partial_sum = kept_partials(
        moff.reshape(-1).astype(jnp.int32),
        oidx.reshape(-1).astype(jnp.int32),
        flow_flat,
        graph_flat,
        n_out,
        layer_count,
        n_g,
    )
    kept_tiles = lax.psum_scatter(partial_sum, "layer", scatter_dimension=0, tiled=True)

    kept_cols = out_coords[0, 0, 0, :, 1]
    squared = kept_tiles * kept_tiles
    local_mass = jnp.sum(squared, axis=1)
    column_total = round_sum(round_sum(local_mass, "row", row_count), "layer", layer_count)
    factor = jnp.float32(row_count * layer_count * tile) / column_total
    flow = squared[kept_cols] * factor[kept_cols][:, None, :]
    return flow.reshape(1, 1, 1, col_tiles, tile, tile)


def solution(mesh):
    in_specs = (
        P("row", "col", "layer", None, None, None),
        P("row", "col", "layer", None, None),
        P("row", "col", "layer", None, None, None),
        P("row", "col", "layer", None, None),
        P("row", "col", "layer", None, None),
    )
    out_specs = P("row", "col", "layer", None, None, None)
    return jax.shard_map(local, mesh=mesh, in_specs=in_specs, out_specs=out_specs, check_vma=False)
```

```python
import functools

import jax
import jax.numpy as jnp
from jax import lax
from jax.experimental import pallas as pl
from jax.experimental.pallas import tpu as pltpu
from jax.sharding import PartitionSpec as P

KA = 4
N_SLOT = 16


def column_kernel(moff_ref, oidx_ref, flow_ref, graph_ref, out_ref, lhs_ref, *, n_q, n_g):
    tile = out_ref.shape[-1]
    n_col = out_ref.shape[0] // n_q

    def column(j, slot):
        for q in range(n_q):
            for g in range(n_g):
                m_off = moff_ref[(j * n_q + q) * n_g + g]
                left = flow_ref[pl.ds(pl.multiple_of(jnp.maximum(m_off, 0), tile), tile), :]
                left = jnp.where(m_off >= 0, left, jnp.zeros_like(left))
                lhs_ref[slot, pl.ds(q * tile, tile), pl.ds(g * tile, tile)] = left
        right = graph_ref[pl.ds(pl.multiple_of(j * n_g * tile, n_g * tile), n_g * tile), :]
        res = jnp.dot(lhs_ref[slot], right, preferred_element_type=jnp.float32)
        for q in range(n_q):
            out_ref[oidx_ref[j * n_q + q]] = res[q * tile : (q + 1) * tile]

    def body(i, carry):
        for k in range(N_SLOT):
            column(N_SLOT * i + k, k)
        return carry

    lax.fori_loop(0, n_col // N_SLOT, body, 0)


def kept_partials(moff, oidx, flow_flat, graph_flat, n_out, n_q, n_g):
    tile = flow_flat.shape[-1]
    kernel = functools.partial(column_kernel, n_q=n_q, n_g=n_g)
    return pl.pallas_call(
        kernel,
        out_shape=jax.ShapeDtypeStruct((n_out, tile, tile), jnp.float32),
        in_specs=[
            pl.BlockSpec(memory_space=pltpu.SMEM),
            pl.BlockSpec(memory_space=pltpu.SMEM),
            pl.BlockSpec(memory_space=pltpu.VMEM),
            pl.BlockSpec(memory_space=pltpu.VMEM),
        ],
        out_specs=pl.BlockSpec(memory_space=pltpu.VMEM),
        scratch_shapes=[
            pltpu.VMEM((N_SLOT, n_q * tile, n_g * tile), jnp.bfloat16),
        ],
        compiler_params=pltpu.CompilerParams(vmem_limit_bytes=48 * 1024 * 1024),
        cost_estimate=pl.CostEstimate(
            flops=2 * n_out * n_g * tile**3,
            transcendentals=0,
            bytes_accessed=2 * (flow_flat.size + graph_flat.size) + 4 * n_out * tile * tile,
        ),
    )(moff, oidx, flow_flat, graph_flat)


def round_sum(x, axis, n):
    parts = [lax.ppermute(x, axis, [(i, i ^ d) for i in range(n)]) for d in range(1, n)]
    return x + sum(parts[1:], parts[0])


def first_two(mask):
    n = mask.shape[-1]
    lo = jnp.argmax(mask, axis=-1).astype(jnp.int32)
    hi = (n - 1 - jnp.argmax(mask[..., ::-1], axis=-1)).astype(jnp.int32)
    return lo, hi


def local(a_tiles, a_coords, b_tiles, b_coords, out_coords):
    tile = a_tiles.shape[-1]
    rows_panel = a_tiles.shape[3]
    col_count = lax.axis_size("col")
    row_count = lax.axis_size("row")
    layer_count = lax.axis_size("layer")
    b_span = KA * col_count // row_count
    quarter = rows_panel // layer_count
    col_tiles = out_coords.shape[3]
    n_b = b_tiles.shape[3]
    my_row = lax.axis_index("row")

    own = b_tiles[0, 0, 0]
    far = lax.ppermute(own, "row", [(i, i ^ 2) for i in range(row_count)])
    near = lax.ppermute(own, "row", [(i, i ^ 1) for i in range(row_count)])
    far_near = lax.ppermute(far, "row", [(i, i ^ 1) for i in range(row_count)])
    graph_parts = [own, near, far, far_near]
    graph_tiles = jnp.concatenate(graph_parts, axis=0)
    graph_coords = lax.all_gather(b_coords[0, 0, 0][None], "row", axis=0, tiled=True)
    flow_tiles = lax.all_gather(a_tiles[0, 0, 0], "col", axis=0, tiled=True)
    flow_coords = lax.all_gather(a_coords[0, 0, 0][None], "col", axis=0, tiled=True)
    kept_all = lax.all_gather(out_coords[0, 0, 0][None], "layer", axis=0, tiled=True)

    n_out = layer_count * col_tiles
    col_ids = jnp.arange(col_tiles, dtype=jnp.int32)
    part_ids = jnp.arange(row_count, dtype=jnp.int32)
    owner_of_part = my_row ^ part_ids
    coords_by_part = graph_coords[owner_of_part]
    in_col = coords_by_part[:, None, :, 1] == col_ids[None, :, None]
    lo, hi = first_two(in_col)
    g_slot = jnp.stack([lo, hi], axis=2)
    g_b0 = jnp.take_along_axis(
        jnp.broadcast_to(coords_by_part[:, None, :, 0], in_col.shape), g_slot, axis=2
    )
    g_inner = owner_of_part[:, None, None] * b_span + g_b0
    g_tile = (part_ids[:, None, None] * n_b + g_slot).transpose(1, 0, 2).reshape(col_tiles, -1)
    g_inner = g_inner.transpose(1, 0, 2).reshape(col_tiles, -1)
    n_g = g_tile.shape[1]

    kept_here = kept_all[:, None, :, 1] == col_ids[None, :, None]
    kept_pos = jnp.argmax(kept_here, axis=2).astype(jnp.int32)
    kept_row0 = jnp.take_along_axis(kept_all[:, :, 0], kept_pos, axis=1)
    q_ids = jnp.arange(layer_count, dtype=jnp.int32)
    kept_row = q_ids[:, None] * quarter + kept_row0
    oidx = jnp.broadcast_to(q_ids[:, None] * col_tiles + col_ids[None, :], (layer_count, col_tiles)).T

    a_rows = flow_coords[:, :, 0]
    a_inner = flow_coords[:, :, 1]
    grp = g_inner // KA
    want = g_inner % KA
    rows_q = kept_row.T
    slot_a = jnp.argmax(
        a_rows[grp[:, None, :], :] == rows_q[:, :, None, None], axis=3
    ).astype(jnp.int32)
    have = a_inner[grp[:, None, :], slot_a] == want[:, None, :]
    moff = jnp.where(have, (grp[:, None, :] * rows_panel + slot_a) * tile, -1)

    flow_flat = flow_tiles.reshape(-1, tile)
    graph_flat = graph_tiles[g_tile.reshape(-1)].reshape(-1, tile)
    partial_sum = kept_partials(
        moff.reshape(-1).astype(jnp.int32),
        oidx.reshape(-1).astype(jnp.int32),
        flow_flat,
        graph_flat,
        n_out,
        layer_count,
        n_g,
    )
    kept_tiles = lax.psum_scatter(partial_sum, "layer", scatter_dimension=0, tiled=True)

    kept_cols = out_coords[0, 0, 0, :, 1]
    squared = kept_tiles * kept_tiles
    local_mass = jnp.sum(squared, axis=1)
    column_total = round_sum(round_sum(local_mass, "row", row_count), "layer", layer_count)
    factor = jnp.float32(row_count * layer_count * tile) / column_total
    flow = squared[kept_cols] * factor[kept_cols][:, None, :]
    return flow.reshape(1, 1, 1, col_tiles, tile, tile)


def solution(mesh):
    in_specs = (
        P("row", "col", "layer", None, None, None),
        P("row", "col", "layer", None, None),
        P("row", "col", "layer", None, None, None),
        P("row", "col", "layer", None, None),
        P("row", "col", "layer", None, None),
    )
    out_specs = P("row", "col", "layer", None, None, None)
    return jax.shard_map(local, mesh=mesh, in_specs=in_specs, out_specs=out_specs, check_vma=False)
```

```python
import functools

import jax
import jax.numpy as jnp
from jax import lax
from jax.experimental import pallas as pl
from jax.experimental.pallas import tpu as pltpu
from jax.sharding import PartitionSpec as P

KA = 4
N_SLOT = 8


def column_kernel(moff_ref, flow_ref, graph_ref, out_ref, lhs_ref, *, n_q, n_g):
    tile = out_ref.shape[-1]
    n_col = out_ref.shape[0] // n_q

    def column(j, slot):
        for q in range(n_q):
            for g in range(n_g):
                m_off = moff_ref[(j * n_q + q) * n_g + g]
                left = flow_ref[pl.ds(pl.multiple_of(jnp.maximum(m_off, 0), tile), tile), :]
                left = jnp.where(m_off >= 0, left, jnp.zeros_like(left))
                lhs_ref[slot, pl.ds(q * tile, tile), pl.ds(g * tile, tile)] = left
        right = graph_ref[pl.ds(pl.multiple_of(j * n_g * tile, n_g * tile), n_g * tile), :]
        res = jnp.dot(lhs_ref[slot], right, preferred_element_type=jnp.float32)
        for q in range(n_q):
            out_ref[q * n_col + j] = res[q * tile : (q + 1) * tile]

    def body(i, carry):
        for k in range(N_SLOT):
            column(N_SLOT * i + k, k)
        return carry

    lax.fori_loop(0, n_col // N_SLOT, body, 0)


def kept_partials(moff, flow_flat, graph_flat, n_out, n_q, n_g):
    tile = flow_flat.shape[-1]
    kernel = functools.partial(column_kernel, n_q=n_q, n_g=n_g)
    return pl.pallas_call(
        kernel,
        out_shape=jax.ShapeDtypeStruct((n_out, tile, tile), jnp.float32),
        in_specs=[
            pl.BlockSpec(memory_space=pltpu.SMEM),
            pl.BlockSpec(memory_space=pltpu.VMEM),
            pl.BlockSpec(memory_space=pltpu.VMEM),
        ],
        out_specs=pl.BlockSpec(memory_space=pltpu.VMEM),
        scratch_shapes=[
            pltpu.VMEM((N_SLOT, n_q * tile, n_g * tile), jnp.bfloat16),
        ],
        compiler_params=pltpu.CompilerParams(vmem_limit_bytes=48 * 1024 * 1024),
        cost_estimate=pl.CostEstimate(
            flops=2 * n_out * n_g * tile**3,
            transcendentals=0,
            bytes_accessed=2 * (flow_flat.size + graph_flat.size) + 4 * n_out * tile * tile,
        ),
    )(moff, flow_flat, graph_flat)


def round_sum(x, axis, n):
    parts = [lax.ppermute(x, axis, [(i, i ^ d) for i in range(n)]) for d in range(1, n)]
    return x + sum(parts[1:], parts[0])


def first_two(mask):
    n = mask.shape[-1]
    lo = jnp.argmax(mask, axis=-1).astype(jnp.int32)
    hi = (n - 1 - jnp.argmax(mask[..., ::-1], axis=-1)).astype(jnp.int32)
    return lo, hi


def local(a_tiles, a_coords, b_tiles, b_coords, out_coords):
    tile = a_tiles.shape[-1]
    rows_panel = a_tiles.shape[3]
    col_count = lax.axis_size("col")
    row_count = lax.axis_size("row")
    layer_count = lax.axis_size("layer")
    b_span = KA * col_count // row_count
    quarter = rows_panel // layer_count
    col_tiles = out_coords.shape[3]
    n_b = b_tiles.shape[3]
    my_row = lax.axis_index("row")

    own = b_tiles[0, 0, 0]
    far = lax.ppermute(own, "row", [(i, i ^ 2) for i in range(row_count)])
    near = lax.ppermute(own, "row", [(i, i ^ 1) for i in range(row_count)])
    far_near = lax.ppermute(far, "row", [(i, i ^ 1) for i in range(row_count)])
    graph_parts = [own, near, far, far_near]
    graph_tiles = jnp.concatenate(graph_parts, axis=0)
    graph_coords = lax.all_gather(b_coords[0, 0, 0][None], "row", axis=0, tiled=True)
    flow_tiles = lax.all_gather(a_tiles[0, 0, 0], "col", axis=0, tiled=True)
    flow_coords = lax.all_gather(a_coords[0, 0, 0][None], "col", axis=0, tiled=True)
    kept_all = lax.all_gather(out_coords[0, 0, 0][None], "layer", axis=0, tiled=True)

    n_out = layer_count * col_tiles
    col_ids = jnp.arange(col_tiles, dtype=jnp.int32)
    part_ids = jnp.arange(row_count, dtype=jnp.int32)
    owner_of_part = my_row ^ part_ids
    coords_by_part = graph_coords[owner_of_part]
    in_col = coords_by_part[:, None, :, 1] == col_ids[None, :, None]
    lo, hi = first_two(in_col)
    g_slot = jnp.stack([lo, hi], axis=2)
    g_b0 = jnp.take_along_axis(
        jnp.broadcast_to(coords_by_part[:, None, :, 0], in_col.shape), g_slot, axis=2
    )
    g_inner = owner_of_part[:, None, None] * b_span + g_b0
    g_tile = (part_ids[:, None, None] * n_b + g_slot).transpose(1, 0, 2).reshape(col_tiles, -1)
    g_inner = g_inner.transpose(1, 0, 2).reshape(col_tiles, -1)
    n_g = g_tile.shape[1]

    kept_here = kept_all[:, None, :, 1] == col_ids[None, :, None]
    kept_pos = jnp.argmax(kept_here, axis=2).astype(jnp.int32)
    kept_row0 = jnp.take_along_axis(kept_all[:, :, 0], kept_pos, axis=1)
    q_ids = jnp.arange(layer_count, dtype=jnp.int32)
    kept_row = q_ids[:, None] * quarter + kept_row0

    a_rows = flow_coords[:, :, 0]
    a_inner = flow_coords[:, :, 1]
    grp = g_inner // KA
    want = g_inner % KA
    rows_q = kept_row.T
    slot_a = jnp.argmax(
        a_rows[grp[:, None, :], :] == rows_q[:, :, None, None], axis=3
    ).astype(jnp.int32)
    have = a_inner[grp[:, None, :], slot_a] == want[:, None, :]
    moff = jnp.where(have, (grp[:, None, :] * rows_panel + slot_a) * tile, -1)

    flow_flat = flow_tiles.reshape(-1, tile)
    graph_flat = graph_tiles[g_tile.reshape(-1)].reshape(-1, tile)
    partial_sum = kept_partials(
        moff.reshape(-1).astype(jnp.int32),
        flow_flat,
        graph_flat,
        n_out,
        layer_count,
        n_g,
    )
    kept_tiles = lax.psum_scatter(partial_sum, "layer", scatter_dimension=0, tiled=True)

    kept_cols = out_coords[0, 0, 0, :, 1]
    squared = kept_tiles * kept_tiles
    local_mass = jnp.sum(squared, axis=1)
    column_total = round_sum(round_sum(local_mass, "row", row_count), "layer", layer_count)
    factor = jnp.float32(row_count * layer_count * tile) / column_total
    flow = squared[kept_cols] * factor[kept_cols][:, None, :]
    return flow.reshape(1, 1, 1, col_tiles, tile, tile)


def solution(mesh):
    in_specs = (
        P("row", "col", "layer", None, None, None),
        P("row", "col", "layer", None, None),
        P("row", "col", "layer", None, None, None),
        P("row", "col", "layer", None, None),
        P("row", "col", "layer", None, None),
    )
    out_specs = P("row", "col", "layer", None, None, None)
    return jax.shard_map(local, mesh=mesh, in_specs=in_specs, out_specs=out_specs, check_vma=False)
```
